1024 devices in a mesh: row: 32 (over y_hi, z), col: 32 (over y_lo, x, core).
Axes of the slice: x: 8, y: 8 (y_hi: 4, y_lo: 2; y = y_hi * 2 + y_lo), z: 8, core: 2. Of those that a mesh axis runs over, the one named last changes fastest.
Arguments:
- object_planes: float32 [2, 8192, 8192], P(None, 'row', 'col'), may hold values from -4 to 4
- probe_modes: float32 [2, 3, 256, 256], replicated, may hold values from -1 to 1
- positions: int32 [32, 32, 1, 2], P('row', 'col'), may hold values from -64 to 64
- amplitudes: float32 [32, 32, 1, 256, 256], P('row', 'col'), may hold values from 0.2 to 4
Outputs:
- object_next: float32 [2, 8192, 8192], P(None, 'row', 'col')
The draws below stay inside these ranges and needn't reach their ends.
Inputs may be any that keep to these rules, and one draw needn't show every extreme that they name: positions[i, j, t] holds the row offset then the column offset of pattern t of tile (i, j); its window may reach up to 64 pixels into the neighbouring tiles.
All inputs are finite; a program needn't handle non-finite values.
Results may differ from the reference program's by a relative error of at most 0.004.
Values sent between devices are 32-bit elements; how exact they have to be, the bound alone decides.
No kernel may reach another device: no remote copies, remote signals or barrier semaphores. Data moves between devices by JAX's collectives and lax.ppermute only.
A program may use at most 32 MiB of HBM per device.

```python
import math
import jax
import jax.numpy as jnp
from jax import lax

TILE = 256
W = 256
M = 64
MODES = 3
PAT_DEV = 1
ITERS = 2
TILES_DOWN = 32
TILES_ACROSS = 32
NY = 8192
NX = 8192


def with_ends(drawn, own_key, least, largest):
    longest = drawn.shape.index(max(drawn.shape))
    spots = []
    for shift in (0, 1):
        where = [jax.random.randint(jax.random.fold_in(own_key, axis), (), 0, length) for axis, length in enumerate(drawn.shape)]
        where[longest] = (where[longest] + shift) % drawn.shape[longest]
        spots.append(tuple(where))
    return drawn.at[spots[0]].set(least).at[spots[1]].set(largest)


def block_scale(stream_key, shape, split, least, top_value):
    def one(position, shards_of):
        heights = jax.random.uniform(jax.random.fold_in(jax.random.fold_in(stream_key, 6), position), (shards_of,), jnp.float32, least / len(split), top_value / len(split))
        return jnp.repeat(jnp.exp(heights), shape[position] // shards_of).reshape((-1,) + (1,) * (len(shape) - position - 1))

    factor_of = one(*split[0])
    for cut in split[1:]:
        factor_of = factor_of * one(*cut)
    return factor_of


def noise(key, dims, scale, most, shards=(), kind=jnp.bfloat16):
    drawn = jax.random.normal(key, dims, jnp.float32) * scale
    if len(shards) > 0:
        drawn = block_scale(key, dims, shards, -0.22, 0.18) * drawn
    return jnp.clip(drawn, min=-most, max=most).astype(kind)


def setup_inputs(seed: int = 0) -> dict:
    keys = jax.random.split(jax.random.key(seed), 5)
    object_planes = noise(keys[0], (2, NY, NX), 0.7, 4.0, ((1, 32), (2, 32)), jnp.float32)
    probe_modes = jnp.clip(jax.random.uniform(keys[1], (2, MODES, W, W), jnp.float32, -1.0, 1.0), -1.0, 1.0)
    positions = with_ends(jax.random.randint(keys[2], (TILES_DOWN, TILES_ACROSS, PAT_DEV, 2), -M, TILE - W + M + 1), jax.random.fold_in(keys[2], 1), -M, TILE - W + M).astype(jnp.int32)
    amplitudes = jnp.clip(jnp.exp(math.log(4.0) - 2.9957323 * jax.random.uniform(keys[3], (TILES_DOWN, TILES_ACROSS, PAT_DEV, W, W), jnp.float32) ** block_scale(keys[3], (TILES_DOWN, TILES_ACROSS, PAT_DEV, W, W), ((0, 32), (1, 32)), -0.2, 0.2)), 0.2, 4.0)
    return {"object_planes": object_planes, "probe_modes": probe_modes, "positions": positions, "amplitudes": amplitudes}


AMPLITUDE_FLOOR = 0.5
EPSILON = 1e-06

def tables(length):
    counter = jnp.arange(length, dtype=jnp.int32)
    product = counter[:, None] * counter[None, :] % length
    phases = product.astype(jnp.float32) * (2.0 * math.pi / length)
    factor = 1.0 / math.sqrt(length)
    return ((jnp.cos(phases) * factor).astype(jnp.bfloat16), (-jnp.sin(phases) * factor).astype(jnp.bfloat16))

def operators(table_re, table_im):
    left_side = jnp.stack([jnp.stack([table_re, -table_im], 1), jnp.stack([table_im, table_re], 1)], 0)
    right_side = jnp.stack([jnp.stack([table_re, table_im], 1), jnp.stack([-table_im, table_re], 1)], 0)
    return (left_side, right_side)

def transform(waves, left_side, right_side):
    half_done = jnp.einsum('puqr,qkrc->pkuc', left_side.astype(jnp.float32), waves.astype(jnp.float32), precision=lax.Precision.HIGHEST).astype(jnp.bfloat16)
    return jnp.einsum('qkrc,qcpv->pkrv', half_done.astype(jnp.float32), right_side.astype(jnp.float32), precision=lax.Precision.HIGHEST)

def pattern_gradient(windows, measured, probe_re, probe_im, forward, inverse):
    obj_re = windows[:, 0][:, None]
    obj_im = windows[:, 1][:, None]
    exit_re = obj_re * probe_re[None] - obj_im * probe_im[None]
    exit_im = obj_re * probe_im[None] + obj_im * probe_re[None]
    exit_waves = jnp.stack([exit_re, exit_im])
    flat_shape = (2, -1) + exit_waves.shape[3:]
    spectrum = transform(exit_waves.reshape(flat_shape).astype(jnp.bfloat16), forward[0], forward[1]).reshape(exit_waves.shape)
    modulus = jnp.sqrt(lax.optimization_barrier(jnp.sum(spectrum * spectrum, axis=(0, 2))))
    scaling = measured / jnp.maximum(modulus, AMPLITUDE_FLOOR)
    corrected = (spectrum * scaling[None, :, None]).astype(jnp.bfloat16).reshape(flat_shape)
    revised = transform(corrected, inverse[0], inverse[1]).reshape(exit_waves.shape)
    residue = revised - exit_waves
    grad_re = lax.optimization_barrier(jnp.sum(probe_re[None] * residue[0] + probe_im[None] * residue[1], axis=1))
    grad_im = lax.optimization_barrier(jnp.sum(probe_re[None] * residue[1] - probe_im[None] * residue[0], axis=1))
    return jnp.stack([grad_re, grad_im], axis=1)

def reference(object_planes, probe_modes, positions, amplitudes):
    table_re, table_im = tables(W)
    forward = operators(table_re, table_im)
    inverse = operators(table_re, -table_im)
    probe_re = probe_modes[0]
    probe_im = probe_modes[1]
    peak_power = jnp.max(lax.optimization_barrier(jnp.sum(probe_modes * probe_modes, axis=(0, 1)))) + EPSILON
    offsets = positions.reshape(-1, 2).astype(jnp.int32)
    measured = amplitudes.reshape(-1, W, W)
    total_patterns = TILES_DOWN * TILES_ACROSS * PAT_DEV
    current = object_planes
    for update in range(ITERS):
        padded = jnp.pad(current, ((0, 0), (M, M), (M, M)))

        def accumulate(gradient, item):
            pattern, offset, single = item
            tile_index = pattern // PAT_DEV
            row_start = (tile_index // TILES_ACROSS * TILE + offset[0] + M).astype(jnp.int32)
            col_start = (tile_index % TILES_ACROSS * TILE + offset[1] + M).astype(jnp.int32)
            anchor = (jnp.zeros((), jnp.int32), row_start, col_start)
            window = lax.dynamic_slice(padded, anchor, (2, W, W))
            change = pattern_gradient(window[None], single[None], probe_re, probe_im, forward, inverse)[0]
            before = lax.dynamic_slice(gradient, anchor, (2, W, W))
            return (lax.dynamic_update_slice(gradient, before + change, anchor), None)
        gradient, unused = lax.scan(accumulate, jnp.zeros_like(padded), (jnp.arange(total_patterns, dtype=jnp.int32), offsets, measured))
        current = current + gradient[:, M:M + NY, M:M + NX] / peak_power
    return current
```

```python
import math

import jax
import jax.numpy as jnp
from jax import lax
from jax.sharding import PartitionSpec as P

W = 256
M = 64
ITERS = 2


AMPLITUDE_FLOOR = 0.5
EPSILON = 1e-06

OFFSETS = [(a, b) for a in (-1, 0, 1) for b in (-1, 0, 1)]


def tables(length):
    counter = jnp.arange(length, dtype=jnp.int32)
    product = counter[:, None] * counter[None, :] % length
    phases = product.astype(jnp.float32) * (2.0 * math.pi / length)
    factor = 1.0 / math.sqrt(length)
    return (
        (jnp.cos(phases) * factor).astype(jnp.bfloat16),
        (-jnp.sin(phases) * factor).astype(jnp.bfloat16),
    )


def operators(table_re, table_im):
    left_side = jnp.stack(
        [jnp.stack([table_re, -table_im], 1), jnp.stack([table_im, table_re], 1)], 0
    )
    right_side = jnp.stack(
        [jnp.stack([table_re, table_im], 1), jnp.stack([-table_im, table_re], 1)], 0
    )
    return (left_side, right_side)


def transform(waves, left_side, right_side):
    half_done = jnp.einsum(
        "puqr,qkrc->pkuc", left_side, waves, preferred_element_type=jnp.float32
    ).astype(jnp.bfloat16)
    return jnp.einsum("qkrc,qcpv->pkrv", half_done, right_side, preferred_element_type=jnp.float32)


def pattern_gradient(windows, measured, probe_re, probe_im, forward, inverse):
    obj_re = windows[:, 0][:, None]
    obj_im = windows[:, 1][:, None]
    exit_re = obj_re * probe_re[None] - obj_im * probe_im[None]
    exit_im = obj_re * probe_im[None] + obj_im * probe_re[None]
    exit_waves = jnp.stack([exit_re, exit_im])
    flat_shape = (2, -1) + exit_waves.shape[3:]
    spectrum = transform(
        exit_waves.reshape(flat_shape).astype(jnp.bfloat16), forward[0], forward[1]
    ).reshape(exit_waves.shape)
    modulus = jnp.sqrt(jnp.sum(spectrum * spectrum, axis=(0, 2)))
    scaling = measured / jnp.maximum(modulus, AMPLITUDE_FLOOR)
    corrected = (spectrum * scaling[None, :, None]).astype(jnp.bfloat16).reshape(flat_shape)
    revised = transform(corrected, inverse[0], inverse[1]).reshape(exit_waves.shape)
    residue = revised - exit_waves
    grad_re = jnp.sum(probe_re[None] * residue[0] + probe_im[None] * residue[1], axis=1)
    grad_im = jnp.sum(probe_re[None] * residue[1] - probe_im[None] * residue[0], axis=1)
    return jnp.stack([grad_re, grad_im], axis=1)


def from_neighbor(x, a, b, rows, cols):
    if b == 0:
        pairs = [(r, r - a) for r in range(rows) if 0 <= r - a < rows]
        return lax.ppermute(x, "row", pairs)
    if a == 0:
        pairs = [(c, c - b) for c in range(cols) if 0 <= c - b < cols]
        return lax.ppermute(x, "col", pairs)
    pairs = [
        (r * cols + c, (r - a) * cols + (c - b))
        for r in range(rows)
        for c in range(cols)
        if 0 <= r - a < rows and 0 <= c - b < cols
    ]
    return lax.ppermute(x, ("row", "col"), pairs)


def overlap(a, step, src_origin, src_size, dst_origin, dst_size):
    low = max(a * step + src_origin, dst_origin)
    high = min(a * step + src_origin + src_size, dst_origin + dst_size)
    shift = a * step + src_origin
    return (low - shift, high - shift), (low - dst_origin, high - dst_origin)


def neighbor_sum(frame, step, src_origin, dst_origin, dst_size):
    rows = lax.axis_size("row")
    cols = lax.axis_size("col")
    src_size = frame.shape[1]
    total = None
    for a, b in OFFSETS:
        (r0, r1), (p0, p1) = overlap(a, step, src_origin, src_size, dst_origin, dst_size)
        (c0, c1), (q0, q1) = overlap(b, step, src_origin, src_size, dst_origin, dst_size)
        piece = frame[:, r0:r1, c0:c1]
        if (a, b) != (0, 0):
            piece = from_neighbor(piece, a, b, rows, cols)
        piece = jnp.pad(piece, ((0, 0), (p0, dst_size - p1), (q0, dst_size - q1)))
        total = piece if total is None else total + piece
    return total


def inside_mask(extent, tile_size):
    rows = lax.axis_size("row")
    cols = lax.axis_size("col")
    i = lax.axis_index("row")
    j = lax.axis_index("col")
    pixel = jnp.arange(extent, dtype=jnp.int32)
    row_ok = ((pixel >= M) | (i > 0)) & ((pixel < tile_size + M) | (i < rows - 1))
    col_ok = ((pixel >= M) | (j > 0)) & ((pixel < tile_size + M) | (j < cols - 1))
    return row_ok[:, None] & col_ok[None, :]


def on_device(object_planes, probe_modes, positions, amplitudes):
    table_re, table_im = tables(W)
    forward = operators(table_re, table_im)
    inverse = operators(table_re, -table_im)
    probe_re = probe_modes[0]
    probe_im = probe_modes[1]
    peak_power = jnp.max(jnp.sum(probe_modes * probe_modes, axis=(0, 1))) + EPSILON
    offsets = positions.reshape(-1, 2)
    measured = amplitudes.reshape(-1, W, W)
    tile_size = object_planes.shape[1]
    extent = tile_size + 2 * M
    place = extent - W
    zero = jnp.zeros((), jnp.int32)
    corner = (zero, offsets[0, 0] + M, offsets[0, 1] + M)
    spread = (zero, place - M - offsets[0, 0], place - M - offsets[0, 1])
    extended = neighbor_sum(object_planes, tile_size, M, 0, extent)
    for update in range(ITERS):
        windows = lax.dynamic_slice(extended, corner, (2, W, W))[None]
        change = pattern_gradient(windows, measured, probe_re, probe_im, forward, inverse)[0]
        padded = jnp.pad(change, ((0, 0), (place, place), (place, place)))
        gathered = lax.dynamic_slice(padded, spread, (2, extent, extent))
        if update + 1 < ITERS:
            total = neighbor_sum(gathered, tile_size, 0, 0, extent)
            mask = inside_mask(extent, tile_size)
            extended = jnp.where(mask[None], extended + total / peak_power, 0.0)
        else:
            total = neighbor_sum(gathered, tile_size, 0, M, tile_size)
            current = extended[:, M : M + tile_size, M : M + tile_size] + total / peak_power
    return current


def solution(mesh):
    in_specs = (
        P(None, "row", "col"),
        P(),
        P("row", "col", None, None),
        P("row", "col", None, None, None),
    )
    out_specs = P(None, "row", "col")
    return jax.shard_map(
        on_device, mesh=mesh, in_specs=in_specs, out_specs=out_specs, check_vma=False
    )
```

```python
import math

import jax
import jax.numpy as jnp
from jax import lax
from jax.sharding import PartitionSpec as P

W = 256
M = 64
ITERS = 2


AMPLITUDE_FLOOR = 0.5
EPSILON = 1e-06


def tables(length):
    counter = jnp.arange(length, dtype=jnp.int32)
    product = counter[:, None] * counter[None, :] % length
    phases = product.astype(jnp.float32) * (2.0 * math.pi / length)
    factor = 1.0 / math.sqrt(length)
    return (
        (jnp.cos(phases) * factor).astype(jnp.bfloat16),
        (-jnp.sin(phases) * factor).astype(jnp.bfloat16),
    )


def operators(table_re, table_im):
    left_side = jnp.stack(
        [jnp.stack([table_re, -table_im], 1), jnp.stack([table_im, table_re], 1)], 0
    )
    right_side = jnp.stack(
        [jnp.stack([table_re, table_im], 1), jnp.stack([-table_im, table_re], 1)], 0
    )
    return (left_side, right_side)


def transform(waves, left_side, right_side):
    half_done = jnp.einsum(
        "puqr,qkrc->pkuc", left_side, waves, preferred_element_type=jnp.float32
    ).astype(jnp.bfloat16)
    return jnp.einsum("qkrc,qcpv->pkrv", half_done, right_side, preferred_element_type=jnp.float32)


def pattern_gradient(windows, measured, probe_re, probe_im, forward, inverse):
    obj_re = windows[:, 0][:, None]
    obj_im = windows[:, 1][:, None]
    exit_re = obj_re * probe_re[None] - obj_im * probe_im[None]
    exit_im = obj_re * probe_im[None] + obj_im * probe_re[None]
    exit_waves = jnp.stack([exit_re, exit_im])
    flat_shape = (2, -1) + exit_waves.shape[3:]
    spectrum = transform(
        exit_waves.reshape(flat_shape).astype(jnp.bfloat16), forward[0], forward[1]
    ).reshape(exit_waves.shape)
    modulus = jnp.sqrt(jnp.sum(spectrum * spectrum, axis=(0, 2)))
    scaling = measured / jnp.maximum(modulus, AMPLITUDE_FLOOR)
    corrected = (spectrum * scaling[None, :, None]).astype(jnp.bfloat16).reshape(flat_shape)
    revised = transform(corrected, inverse[0], inverse[1]).reshape(exit_waves.shape)
    residue = revised - exit_waves
    grad_re = jnp.sum(probe_re[None] * residue[0] + probe_im[None] * residue[1], axis=1)
    grad_im = jnp.sum(probe_re[None] * residue[1] - probe_im[None] * residue[0], axis=1)
    return jnp.stack([grad_re, grad_im], axis=1)


def from_neighbor(x, axis, a):
    count = lax.axis_size(axis)
    pairs = [(r, r - a) for r in range(count) if 0 <= r - a < count]
    return lax.ppermute(x, axis, pairs)


def neighbor_sum(frame, axis, dim, step, src_origin, dst_origin, dst_size):
    src_size = frame.shape[dim]
    total = None
    for a in (-1, 0, 1):
        low = max(a * step + src_origin, dst_origin)
        high = min(a * step + src_origin + src_size, dst_origin + dst_size)
        shift = a * step + src_origin
        piece = lax.slice_in_dim(frame, low - shift, high - shift, axis=dim)
        if a != 0:
            piece = from_neighbor(piece, axis, a)
        widths = [(0, 0)] * frame.ndim
        widths[dim] = (low - dst_origin, dst_origin + dst_size - high)
        piece = jnp.pad(piece, widths)
        total = piece if total is None else total + piece
    return total


def inside_mask(extent, tile_size):
    rows = lax.axis_size("row")
    cols = lax.axis_size("col")
    i = lax.axis_index("row")
    j = lax.axis_index("col")
    pixel = jnp.arange(extent, dtype=jnp.int32)
    row_ok = ((pixel >= M) | (i > 0)) & ((pixel < tile_size + M) | (i < rows - 1))
    col_ok = ((pixel >= M) | (j > 0)) & ((pixel < tile_size + M) | (j < cols - 1))
    return row_ok[:, None] & col_ok[None, :]


def on_device(object_planes, probe_modes, positions, amplitudes):
    table_re, table_im = tables(W)
    forward = operators(table_re, table_im)
    inverse = operators(table_re, -table_im)
    probe_re = probe_modes[0]
    probe_im = probe_modes[1]
    peak_power = jnp.max(jnp.sum(probe_modes * probe_modes, axis=(0, 1))) + EPSILON
    offsets = positions.reshape(-1, 2)
    measured = amplitudes.reshape(-1, W, W)
    tile_size = object_planes.shape[1]
    extent = tile_size + 2 * M
    place = extent - W
    zero = jnp.zeros((), jnp.int32)
    corner = (zero, offsets[0, 0] + M, offsets[0, 1] + M)
    spread = (zero, place - M - offsets[0, 0], place - M - offsets[0, 1])
    extended = neighbor_sum(object_planes, "row", 1, tile_size, M, 0, extent)
    extended = neighbor_sum(extended, "col", 2, tile_size, M, 0, extent)
    for update in range(ITERS):
        windows = lax.dynamic_slice(extended, corner, (2, W, W))[None]
        change = pattern_gradient(windows, measured, probe_re, probe_im, forward, inverse)[0]
        padded = jnp.pad(change, ((0, 0), (place, place), (place, place)))
        gathered = lax.dynamic_slice(padded, spread, (2, extent, extent))
        if update + 1 < ITERS:
            total = neighbor_sum(gathered, "col", 2, tile_size, 0, 0, extent)
            total = neighbor_sum(total, "row", 1, tile_size, 0, 0, extent)
            mask = inside_mask(extent, tile_size)
            extended = jnp.where(mask[None], extended + total / peak_power, 0.0)
        else:
            total = neighbor_sum(gathered, "col", 2, tile_size, 0, M, tile_size)
            total = neighbor_sum(total, "row", 1, tile_size, 0, M, tile_size)
            current = extended[:, M : M + tile_size, M : M + tile_size] + total / peak_power
    return current


def solution(mesh):
    in_specs = (
        P(None, "row", "col"),
        P(),
        P("row", "col", None, None),
        P("row", "col", None, None, None),
    )
    out_specs = P(None, "row", "col")
    return jax.shard_map(
        on_device, mesh=mesh, in_specs=in_specs, out_specs=out_specs, check_vma=False
    )
```

```python
import math

import jax
import jax.numpy as jnp
from jax import lax
from jax.experimental import pallas as pl
from jax.experimental.pallas import tpu as pltpu
from jax.sharding import PartitionSpec as P

W = 256
M = 64
ITERS = 2


AMPLITUDE_FLOOR = 0.5
EPSILON = 1e-06


def tables(length):
    counter = jnp.arange(length, dtype=jnp.int32)
    product = counter[:, None] * counter[None, :] % length
    phases = product.astype(jnp.float32) * (2.0 * math.pi / length)
    factor = 1.0 / math.sqrt(length)
    return (
        (jnp.cos(phases) * factor).astype(jnp.bfloat16),
        (-jnp.sin(phases) * factor).astype(jnp.bfloat16),
    )


INTERPRET = False


def gradient_kernel(window_ref, probe_ref, measured_ref, table_re_ref, table_im_ref, out_ref, spectrum_ref):
    modes = probe_ref.shape[1]
    table_re = table_re_ref[...]
    table_im = table_im_ref[...]

    def product(left, right):
        return jnp.dot(left, right, preferred_element_type=jnp.float32)

    def exit_wave(k):
        obj_re = window_ref[0]
        obj_im = window_ref[1]
        probe_re = probe_ref[0, k]
        probe_im = probe_ref[1, k]
        return obj_re * probe_re - obj_im * probe_im, obj_re * probe_im + obj_im * probe_re

    power = None
    for k in range(modes):
        exit_re, exit_im = exit_wave(k)
        exit_re = exit_re.astype(jnp.bfloat16)
        exit_im = exit_im.astype(jnp.bfloat16)
        half_re = (product(table_re, exit_re) - product(table_im, exit_im)).astype(jnp.bfloat16)
        half_im = (product(table_im, exit_re) + product(table_re, exit_im)).astype(jnp.bfloat16)
        spec_re = product(half_re, table_re) - product(half_im, table_im)
        spec_im = product(half_re, table_im) + product(half_im, table_re)
        spectrum_ref[0, k] = spec_re
        spectrum_ref[1, k] = spec_im
        term = spec_re * spec_re + spec_im * spec_im
        power = term if power is None else power + term
    scaling = measured_ref[...] / jnp.maximum(jnp.sqrt(power), AMPLITUDE_FLOOR)
    grad_re = None
    grad_im = None
    for k in range(modes):
        fixed_re = (spectrum_ref[0, k] * scaling).astype(jnp.bfloat16)
        fixed_im = (spectrum_ref[1, k] * scaling).astype(jnp.bfloat16)
        back_re = (product(table_re, fixed_re) + product(table_im, fixed_im)).astype(jnp.bfloat16)
        back_im = (product(table_re, fixed_im) - product(table_im, fixed_re)).astype(jnp.bfloat16)
        revised_re = product(back_re, table_re) + product(back_im, table_im)
        revised_im = product(back_im, table_re) - product(back_re, table_im)
        exit_re, exit_im = exit_wave(k)
        residue_re = revised_re - exit_re
        residue_im = revised_im - exit_im
        probe_re = probe_ref[0, k]
        probe_im = probe_ref[1, k]
        part_re = probe_re * residue_re + probe_im * residue_im
        part_im = probe_re * residue_im - probe_im * residue_re
        grad_re = part_re if grad_re is None else grad_re + part_re
        grad_im = part_im if grad_im is None else grad_im + part_im
    out_ref[0] = grad_re
    out_ref[1] = grad_im


def pattern_gradient(window, measured, probe_modes, table_re, table_im):
    _, modes, rows, cols = probe_modes.shape
    return pl.pallas_call(
        gradient_kernel,
        out_shape=jax.ShapeDtypeStruct((2, rows, cols), jnp.float32),
        scratch_shapes=[pltpu.VMEM((2, modes, rows, cols), jnp.float32)],
        interpret=INTERPRET,
    )(window, probe_modes, measured, table_re, table_im)


def from_neighbor(x, axis, a):
    count = lax.axis_size(axis)
    pairs = [(r, r - a) for r in range(count) if 0 <= r - a < count]
    return lax.ppermute(x, axis, pairs)


def neighbor_sum(frame, axis, dim, step, src_origin, dst_origin, dst_size):
    src_size = frame.shape[dim]
    total = None
    for a in (-1, 0, 1):
        low = max(a * step + src_origin, dst_origin)
        high = min(a * step + src_origin + src_size, dst_origin + dst_size)
        shift = a * step + src_origin
        piece = lax.slice_in_dim(frame, low - shift, high - shift, axis=dim)
        if a != 0:
            piece = from_neighbor(piece, axis, a)
        widths = [(0, 0)] * frame.ndim
        widths[dim] = (low - dst_origin, dst_origin + dst_size - high)
        piece = jnp.pad(piece, widths)
        total = piece if total is None else total + piece
    return total


def inside_mask(extent, tile_size):
    rows = lax.axis_size("row")
    cols = lax.axis_size("col")
    i = lax.axis_index("row")
    j = lax.axis_index("col")
    pixel = jnp.arange(extent, dtype=jnp.int32)
    row_ok = ((pixel >= M) | (i > 0)) & ((pixel < tile_size + M) | (i < rows - 1))
    col_ok = ((pixel >= M) | (j > 0)) & ((pixel < tile_size + M) | (j < cols - 1))
    return row_ok[:, None] & col_ok[None, :]


def on_device(object_planes, probe_modes, positions, amplitudes):
    table_re, table_im = tables(W)
    peak_power = jnp.max(jnp.sum(probe_modes * probe_modes, axis=(0, 1))) + EPSILON
    offsets = positions.reshape(-1, 2)
    measured = amplitudes.reshape(-1, W, W)
    tile_size = object_planes.shape[1]
    extent = tile_size + 2 * M
    place = extent - W
    zero = jnp.zeros((), jnp.int32)
    corner = (zero, offsets[0, 0] + M, offsets[0, 1] + M)
    spread = (zero, place - M - offsets[0, 0], place - M - offsets[0, 1])
    extended = neighbor_sum(object_planes, "row", 1, tile_size, M, 0, extent)
    extended = neighbor_sum(extended, "col", 2, tile_size, M, 0, extent)
    for update in range(ITERS):
        window = lax.dynamic_slice(extended, corner, (2, W, W))
        change = pattern_gradient(window, measured[0], probe_modes, table_re, table_im)
        padded = jnp.pad(change, ((0, 0), (place, place), (place, place)))
        gathered = lax.dynamic_slice(padded, spread, (2, extent, extent))
        if update + 1 < ITERS:
            total = neighbor_sum(gathered, "col", 2, tile_size, 0, 0, extent)
            total = neighbor_sum(total, "row", 1, tile_size, 0, 0, extent)
            mask = inside_mask(extent, tile_size)
            extended = jnp.where(mask[None], extended + total / peak_power, 0.0)
        else:
            total = neighbor_sum(gathered, "col", 2, tile_size, 0, M, tile_size)
            total = neighbor_sum(total, "row", 1, tile_size, 0, M, tile_size)
            current = extended[:, M : M + tile_size, M : M + tile_size] + total / peak_power
    return current


def solution(mesh):
    in_specs = (
        P(None, "row", "col"),
        P(),
        P("row", "col", None, None),
        P("row", "col", None, None, None),
    )
    out_specs = P(None, "row", "col")
    return jax.shard_map(
        on_device, mesh=mesh, in_specs=in_specs, out_specs=out_specs, check_vma=False
    )
```

```python
import math

import jax
import jax.numpy as jnp
from jax import lax
from jax.experimental import pallas as pl
from jax.experimental.pallas import tpu as pltpu
from jax.sharding import PartitionSpec as P

W = 256
M = 64
ITERS = 2


AMPLITUDE_FLOOR = 0.5
EPSILON = 1e-06


def tables(length):
    counter = jnp.arange(length, dtype=jnp.int32)
    product = counter[:, None] * counter[None, :] % length
    phases = product.astype(jnp.float32) * (2.0 * math.pi / length)
    factor = 1.0 / math.sqrt(length)
    return (
        (jnp.cos(phases) * factor).astype(jnp.bfloat16),
        (-jnp.sin(phases) * factor).astype(jnp.bfloat16),
    )


INTERPRET = False


def gradient_kernel(window_ref, probe_ref, measured_ref, table_re_ref, table_im_ref, out_ref, spectrum_ref):
    modes = probe_ref.shape[1]
    table_re = table_re_ref[...]
    table_im = table_im_ref[...]

    def product(left, right):
        return jnp.dot(left, right, preferred_element_type=jnp.float32)

    def exit_wave(k):
        obj_re = window_ref[0]
        obj_im = window_ref[1]
        probe_re = probe_ref[0, k]
        probe_im = probe_ref[1, k]
        return obj_re * probe_re - obj_im * probe_im, obj_re * probe_im + obj_im * probe_re

    power = None
    for k in range(modes):
        exit_re, exit_im = exit_wave(k)
        exit_re = exit_re.astype(jnp.bfloat16)
        exit_im = exit_im.astype(jnp.bfloat16)
        half_re = (product(table_re, exit_re) - product(table_im, exit_im)).astype(jnp.bfloat16)
        half_im = (product(table_im, exit_re) + product(table_re, exit_im)).astype(jnp.bfloat16)
        spec_re = product(half_re, table_re) - product(half_im, table_im)
        spec_im = product(half_re, table_im) + product(half_im, table_re)
        spectrum_ref[0, k] = spec_re
        spectrum_ref[1, k] = spec_im
        term = spec_re * spec_re + spec_im * spec_im
        power = term if power is None else power + term
    scaling = measured_ref[...] / jnp.maximum(jnp.sqrt(power), AMPLITUDE_FLOOR)
    grad_re = None
    grad_im = None
    for k in range(modes):
        fixed_re = (spectrum_ref[0, k] * scaling).astype(jnp.bfloat16)
        fixed_im = (spectrum_ref[1, k] * scaling).astype(jnp.bfloat16)
        back_re = (product(table_re, fixed_re) + product(table_im, fixed_im)).astype(jnp.bfloat16)
        back_im = (product(table_re, fixed_im) - product(table_im, fixed_re)).astype(jnp.bfloat16)
        revised_re = product(back_re, table_re) + product(back_im, table_im)
        revised_im = product(back_im, table_re) - product(back_re, table_im)
        exit_re, exit_im = exit_wave(k)
        residue_re = revised_re - exit_re
        residue_im = revised_im - exit_im
        probe_re = probe_ref[0, k]
        probe_im = probe_ref[1, k]
        part_re = probe_re * residue_re + probe_im * residue_im
        part_im = probe_re * residue_im - probe_im * residue_re
        grad_re = part_re if grad_re is None else grad_re + part_re
        grad_im = part_im if grad_im is None else grad_im + part_im
    out_ref[0] = grad_re
    out_ref[1] = grad_im


def pattern_gradient(window, measured, probe_modes, table_re, table_im):
    _, modes, rows, cols = probe_modes.shape
    return pl.pallas_call(
        gradient_kernel,
        out_shape=jax.ShapeDtypeStruct((2, rows, cols), jnp.float32),
        scratch_shapes=[pltpu.VMEM((2, modes, rows, cols), jnp.float32)],
        interpret=INTERPRET,
    )(window, probe_modes, measured, table_re, table_im)


def swap_with_neighbors(to_low, to_high, axis):
    count = lax.axis_size(axis)
    where = lax.axis_index(axis)
    odd = where % 2 == 1
    first = [[2 * k, 2 * k + 1] for k in range(count // 2)]
    second = [[2 * k + 1, 2 * k + 2] for k in range(count // 2 - 1)] + [[0, count - 1]]
    got = lax.all_gather(jnp.where(odd, to_low, to_high), axis, axis_index_groups=first)
    partner_first = jnp.where(odd, got[0], got[1])
    got = lax.all_gather(jnp.where(odd, to_high, to_low), axis, axis_index_groups=second)
    second_pos = jnp.where(where == 0, 0, jnp.where(where == count - 1, 1, (where + 1) % 2))
    partner_second = jnp.where(second_pos == 0, got[1], got[0])
    from_low = jnp.where(odd, partner_first, partner_second)
    from_high = jnp.where(odd, partner_second, partner_first)
    from_low = jnp.where(where > 0, from_low, 0.0)
    from_high = jnp.where(where < count - 1, from_high, 0.0)
    return from_low, from_high


def neighbor_sum(frame, axis, dim, step, src_origin, dst_origin, dst_size):
    src_size = frame.shape[dim]
    pieces = {}
    for a in (-1, 0, 1):
        low = max(a * step + src_origin, dst_origin)
        high = min(a * step + src_origin + src_size, dst_origin + dst_size)
        shift = a * step + src_origin
        widths = [(0, 0)] * frame.ndim
        widths[dim] = (low - dst_origin, dst_origin + dst_size - high)
        pieces[a] = (lax.slice_in_dim(frame, low - shift, high - shift, axis=dim), widths)
    from_low, from_high = swap_with_neighbors(pieces[1][0], pieces[-1][0], axis)
    total = jnp.pad(pieces[0][0], pieces[0][1])
    total = total + jnp.pad(from_low, pieces[-1][1])
    total = total + jnp.pad(from_high, pieces[1][1])
    return total


def inside_mask(extent, tile_size):
    rows = lax.axis_size("row")
    cols = lax.axis_size("col")
    i = lax.axis_index("row")
    j = lax.axis_index("col")
    pixel = jnp.arange(extent, dtype=jnp.int32)
    row_ok = ((pixel >= M) | (i > 0)) & ((pixel < tile_size + M) | (i < rows - 1))
    col_ok = ((pixel >= M) | (j > 0)) & ((pixel < tile_size + M) | (j < cols - 1))
    return row_ok[:, None] & col_ok[None, :]


def on_device(object_planes, probe_modes, positions, amplitudes):
    table_re, table_im = tables(W)
    peak_power = jnp.max(jnp.sum(probe_modes * probe_modes, axis=(0, 1))) + EPSILON
    offsets = positions.reshape(-1, 2)
    measured = amplitudes.reshape(-1, W, W)
    tile_size = object_planes.shape[1]
    extent = tile_size + 2 * M
    place = extent - W
    zero = jnp.zeros((), jnp.int32)
    corner = (zero, offsets[0, 0] + M, offsets[0, 1] + M)
    spread = (zero, place - M - offsets[0, 0], place - M - offsets[0, 1])
    extended = neighbor_sum(object_planes, "row", 1, tile_size, M, 0, extent)
    extended = neighbor_sum(extended, "col", 2, tile_size, M, 0, extent)
    for update in range(ITERS):
        window = lax.dynamic_slice(extended, corner, (2, W, W))
        change = pattern_gradient(window, measured[0], probe_modes, table_re, table_im)
        padded = jnp.pad(change, ((0, 0), (place, place), (place, place)))
        gathered = lax.dynamic_slice(padded, spread, (2, extent, extent))
        if update + 1 < ITERS:
            total = neighbor_sum(gathered, "col", 2, tile_size, 0, 0, extent)
            total = neighbor_sum(total, "row", 1, tile_size, 0, 0, extent)
            mask = inside_mask(extent, tile_size)
            extended = jnp.where(mask[None], extended + total / peak_power, 0.0)
        else:
            total = neighbor_sum(gathered, "col", 2, tile_size, 0, M, tile_size)
            total = neighbor_sum(total, "row", 1, tile_size, 0, M, tile_size)
            current = extended[:, M : M + tile_size, M : M + tile_size] + total / peak_power
    return current


def solution(mesh):
    in_specs = (
        P(None, "row", "col"),
        P(),
        P("row", "col", None, None),
        P("row", "col", None, None, None),
    )
    out_specs = P(None, "row", "col")
    return jax.shard_map(
        on_device, mesh=mesh, in_specs=in_specs, out_specs=out_specs, check_vma=False
    )
```

```python
import math

import jax
import jax.numpy as jnp
from jax import lax
from jax.experimental import pallas as pl
from jax.experimental.pallas import tpu as pltpu
from jax.sharding import PartitionSpec as P

W = 256
M = 64
ITERS = 2


AMPLITUDE_FLOOR = 0.5
EPSILON = 1e-06


def tables(length):
    counter = jnp.arange(length, dtype=jnp.int32)
    product = counter[:, None] * counter[None, :] % length
    phases = product.astype(jnp.float32) * (2.0 * math.pi / length)
    factor = 1.0 / math.sqrt(length)
    return (
        (jnp.cos(phases) * factor).astype(jnp.bfloat16),
        (-jnp.sin(phases) * factor).astype(jnp.bfloat16),
    )


INTERPRET = False


def operators(table_re, table_im):
    left_side = jnp.concatenate(
        [jnp.concatenate([table_re, -table_im], 1), jnp.concatenate([table_im, table_re], 1)], 0
    )
    right_side = jnp.concatenate(
        [jnp.concatenate([table_re, table_im], 1), jnp.concatenate([-table_im, table_re], 1)], 0
    )
    return left_side, right_side


def gradient_kernel(window_ref, probe_ref, measured_ref, fwd_left_ref, fwd_right_ref,
                    inv_left_ref, inv_right_ref, out_ref, spectrum_ref):
    modes = probe_ref.shape[1]
    size = probe_ref.shape[3]

    def product(left, right):
        return jnp.dot(left, right, preferred_element_type=jnp.float32)

    def stage(left_ref, right_ref, wave_re, wave_im):
        stacked = jnp.concatenate([wave_re, wave_im], axis=0)
        half = product(left_ref[...], stacked).astype(jnp.bfloat16)
        side = jnp.concatenate([half[:size], half[size:]], axis=1)
        done = product(side, right_ref[...])
        return done[:, :size], done[:, size:]

    def exit_wave(k):
        obj_re = window_ref[0]
        obj_im = window_ref[1]
        probe_re = probe_ref[0, k]
        probe_im = probe_ref[1, k]
        return obj_re * probe_re - obj_im * probe_im, obj_re * probe_im + obj_im * probe_re

    power = None
    for k in range(modes):
        exit_re, exit_im = exit_wave(k)
        spec_re, spec_im = stage(
            fwd_left_ref, fwd_right_ref, exit_re.astype(jnp.bfloat16), exit_im.astype(jnp.bfloat16)
        )
        spectrum_ref[0, k] = spec_re
        spectrum_ref[1, k] = spec_im
        term = spec_re * spec_re + spec_im * spec_im
        power = term if power is None else power + term
    scaling = measured_ref[...] / jnp.maximum(jnp.sqrt(power), AMPLITUDE_FLOOR)
    grad_re = None
    grad_im = None
    for k in range(modes):
        fixed_re = (spectrum_ref[0, k] * scaling).astype(jnp.bfloat16)
        fixed_im = (spectrum_ref[1, k] * scaling).astype(jnp.bfloat16)
        revised_re, revised_im = stage(inv_left_ref, inv_right_ref, fixed_re, fixed_im)
        exit_re, exit_im = exit_wave(k)
        residue_re = revised_re - exit_re
        residue_im = revised_im - exit_im
        probe_re = probe_ref[0, k]
        probe_im = probe_ref[1, k]
        part_re = probe_re * residue_re + probe_im * residue_im
        part_im = probe_re * residue_im - probe_im * residue_re
        grad_re = part_re if grad_re is None else grad_re + part_re
        grad_im = part_im if grad_im is None else grad_im + part_im
    out_ref[0] = grad_re
    out_ref[1] = grad_im


def pattern_gradient(window, measured, probe_modes, forward, inverse):
    _, modes, rows, cols = probe_modes.shape
    return pl.pallas_call(
        gradient_kernel,
        out_shape=jax.ShapeDtypeStruct((2, rows, cols), jnp.float32),
        scratch_shapes=[pltpu.VMEM((2, modes, rows, cols), jnp.float32)],
        interpret=INTERPRET,
    )(window, probe_modes, measured, forward[0], forward[1], inverse[0], inverse[1])


def from_neighbor(x, axis, a):
    count = lax.axis_size(axis)
    pairs = [(r, r - a) for r in range(count) if 0 <= r - a < count]
    return lax.ppermute(x, axis, pairs)


def neighbor_sum(frame, axis, dim, step, src_origin, dst_origin, dst_size):
    src_size = frame.shape[dim]
    total = None
    for a in (-1, 0, 1):
        low = max(a * step + src_origin, dst_origin)
        high = min(a * step + src_origin + src_size, dst_origin + dst_size)
        shift = a * step + src_origin
        piece = lax.slice_in_dim(frame, low - shift, high - shift, axis=dim)
        if a != 0:
            piece = from_neighbor(piece, axis, a)
        widths = [(0, 0)] * frame.ndim
        widths[dim] = (low - dst_origin, dst_origin + dst_size - high)
        piece = jnp.pad(piece, widths)
        total = piece if total is None else total + piece
    return total


def inside_mask(extent, tile_size):
    rows = lax.axis_size("row")
    cols = lax.axis_size("col")
    i = lax.axis_index("row")
    j = lax.axis_index("col")
    pixel = jnp.arange(extent, dtype=jnp.int32)
    row_ok = ((pixel >= M) | (i > 0)) & ((pixel < tile_size + M) | (i < rows - 1))
    col_ok = ((pixel >= M) | (j > 0)) & ((pixel < tile_size + M) | (j < cols - 1))
    return row_ok[:, None] & col_ok[None, :]


def on_device(object_planes, probe_modes, positions, amplitudes):
    table_re, table_im = tables(W)
    forward = operators(table_re, table_im)
    inverse = operators(table_re, -table_im)
    peak_power = jnp.max(jnp.sum(probe_modes * probe_modes, axis=(0, 1))) + EPSILON
    offsets = positions.reshape(-1, 2)
    measured = amplitudes.reshape(-1, W, W)
    tile_size = object_planes.shape[1]
    extent = tile_size + 2 * M
    place = extent - W
    zero = jnp.zeros((), jnp.int32)
    corner = (zero, offsets[0, 0] + M, offsets[0, 1] + M)
    spread = (zero, place - M - offsets[0, 0], place - M - offsets[0, 1])
    extended = neighbor_sum(object_planes, "row", 1, tile_size, M, 0, extent)
    extended = neighbor_sum(extended, "col", 2, tile_size, M, 0, extent)
    for update in range(ITERS):
        window = lax.dynamic_slice(extended, corner, (2, W, W))
        change = pattern_gradient(window, measured[0], probe_modes, forward, inverse)
        padded = jnp.pad(change, ((0, 0), (place, place), (place, place)))
        gathered = lax.dynamic_slice(padded, spread, (2, extent, extent))
        if update + 1 < ITERS:
            total = neighbor_sum(gathered, "col", 2, tile_size, 0, 0, extent)
            total = neighbor_sum(total, "row", 1, tile_size, 0, 0, extent)
            mask = inside_mask(extent, tile_size)
            extended = jnp.where(mask[None], extended + total / peak_power, 0.0)
        else:
            total = neighbor_sum(gathered, "col", 2, tile_size, 0, M, tile_size)
            total = neighbor_sum(total, "row", 1, tile_size, 0, M, tile_size)
            current = extended[:, M : M + tile_size, M : M + tile_size] + total / peak_power
    return current


def solution(mesh):
    in_specs = (
        P(None, "row", "col"),
        P(),
        P("row", "col", None, None),
        P("row", "col", None, None, None),
    )
    out_specs = P(None, "row", "col")
    return jax.shard_map(
        on_device, mesh=mesh, in_specs=in_specs, out_specs=out_specs, check_vma=False
    )
```

```python
import math

import jax
import jax.numpy as jnp
from jax import lax
from jax.experimental import pallas as pl
from jax.experimental.pallas import tpu as pltpu
from jax.sharding import PartitionSpec as P

W = 256
M = 64
ITERS = 2


AMPLITUDE_FLOOR = 0.5
EPSILON = 1e-06


def tables(length):
    counter = jnp.arange(length, dtype=jnp.int32)
    product = counter[:, None] * counter[None, :] % length
    phases = product.astype(jnp.float32) * (2.0 * math.pi / length)
    factor = 1.0 / math.sqrt(length)
    return (
        (jnp.cos(phases) * factor).astype(jnp.bfloat16),
        (-jnp.sin(phases) * factor).astype(jnp.bfloat16),
    )


INTERPRET = False


def gradient_kernel(window_ref, probe_ref, measured_ref, table_re_ref, table_im_ref, out_ref, spectrum_ref):
    modes = probe_ref.shape[1]
    table_re = table_re_ref[...]
    table_im = table_im_ref[...]

    def product(left, right):
        return jnp.dot(left, right, preferred_element_type=jnp.float32)

    def exit_wave(k):
        obj_re = window_ref[0]
        obj_im = window_ref[1]
        probe_re = probe_ref[0, k]
        probe_im = probe_ref[1, k]
        return obj_re * probe_re - obj_im * probe_im, obj_re * probe_im + obj_im * probe_re

    power = None
    for k in range(modes):
        exit_re, exit_im = exit_wave(k)
        exit_re = exit_re.astype(jnp.bfloat16)
        exit_im = exit_im.astype(jnp.bfloat16)
        half_re = (product(table_re, exit_re) - product(table_im, exit_im)).astype(jnp.bfloat16)
        half_im = (product(table_im, exit_re) + product(table_re, exit_im)).astype(jnp.bfloat16)
        spec_re = product(half_re, table_re) - product(half_im, table_im)
        spec_im = product(half_re, table_im) + product(half_im, table_re)
        spectrum_ref[0, k] = spec_re
        spectrum_ref[1, k] = spec_im
        term = spec_re * spec_re + spec_im * spec_im
        power = term if power is None else power + term
    scaling = measured_ref[...] / jnp.maximum(jnp.sqrt(power), AMPLITUDE_FLOOR)
    grad_re = None
    grad_im = None
    for k in range(modes):
        fixed_re = (spectrum_ref[0, k] * scaling).astype(jnp.bfloat16)
        fixed_im = (spectrum_ref[1, k] * scaling).astype(jnp.bfloat16)
        back_re = (product(table_re, fixed_re) + product(table_im, fixed_im)).astype(jnp.bfloat16)
        back_im = (product(table_re, fixed_im) - product(table_im, fixed_re)).astype(jnp.bfloat16)
        revised_re = product(back_re, table_re) + product(back_im, table_im)
        revised_im = product(back_im, table_re) - product(back_re, table_im)
        exit_re, exit_im = exit_wave(k)
        residue_re = revised_re - exit_re
        residue_im = revised_im - exit_im
        probe_re = probe_ref[0, k]
        probe_im = probe_ref[1, k]
        part_re = probe_re * residue_re + probe_im * residue_im
        part_im = probe_re * residue_im - probe_im * residue_re
        grad_re = part_re if grad_re is None else grad_re + part_re
        grad_im = part_im if grad_im is None else grad_im + part_im
    out_ref[0] = grad_re
    out_ref[1] = grad_im


def pattern_gradient(window, measured, probe_modes, table_re, table_im):
    _, modes, rows, cols = probe_modes.shape
    return pl.pallas_call(
        gradient_kernel,
        out_shape=jax.ShapeDtypeStruct((2, rows, cols), jnp.float32),
        scratch_shapes=[pltpu.VMEM((2, modes, rows, cols), jnp.float32)],
        interpret=INTERPRET,
    )(window, probe_modes, measured, table_re, table_im)


def from_neighbor(x, axis, a):
    count = lax.axis_size(axis)
    pairs = [(r, r - a) for r in range(count) if 0 <= r - a < count]
    return lax.ppermute(x, axis, pairs)


def neighbor_sum(frame, axis, dim, step, src_origin, dst_origin, dst_size):
    src_size = frame.shape[dim]
    total = None
    for a in (-1, 0, 1):
        low = max(a * step + src_origin, dst_origin)
        high = min(a * step + src_origin + src_size, dst_origin + dst_size)
        shift = a * step + src_origin
        piece = lax.slice_in_dim(frame, low - shift, high - shift, axis=dim)
        if a != 0:
            piece = from_neighbor(piece, axis, a)
        widths = [(0, 0)] * frame.ndim
        widths[dim] = (low - dst_origin, dst_origin + dst_size - high)
        piece = jnp.pad(piece, widths)
        total = piece if total is None else total + piece
    return total


def rows_from_neighbors(change, offset, tile_size, extent):
    reach = 2 * M
    size = change.shape[1]
    tag = jnp.broadcast_to(
        jnp.stack([offset[0], offset[1]] + [offset[0]] * 6).astype(jnp.float32)[None, :, None],
        (2, 8, change.shape[2]),
    )
    to_low = jnp.concatenate([change[:, :reach], tag], axis=1)
    to_high = jnp.concatenate([change[:, size - reach :], tag], axis=1)
    from_high = from_neighbor(to_low, "row", 1)
    from_low = from_neighbor(to_high, "row", -1)
    place = extent - W
    total = None
    for got, low_side in ((from_high, False), (from_low, True)):
        strip = got[:, :reach]
        row_at = got[0, reach, 0].astype(jnp.int32)
        col_at = got[0, reach + 1, 0].astype(jnp.int32)
        if low_side:
            top = row_at + M + size - reach - tile_size
            widths = (0, extent)
        else:
            top = row_at + M + tile_size
            widths = (extent, 0)
        padded = jnp.pad(strip, ((0, 0), widths, (place, place)))
        start = widths[0] - top
        piece = lax.dynamic_slice(
            padded, (jnp.zeros((), jnp.int32), start, place - M - col_at), (2, extent, extent)
        )
        total = piece if total is None else total + piece
    return total


def inside_mask(extent, tile_size):
    rows = lax.axis_size("row")
    cols = lax.axis_size("col")
    i = lax.axis_index("row")
    j = lax.axis_index("col")
    pixel = jnp.arange(extent, dtype=jnp.int32)
    row_ok = ((pixel >= M) | (i > 0)) & ((pixel < tile_size + M) | (i < rows - 1))
    col_ok = ((pixel >= M) | (j > 0)) & ((pixel < tile_size + M) | (j < cols - 1))
    return row_ok[:, None] & col_ok[None, :]


def on_device(object_planes, probe_modes, positions, amplitudes):
    table_re, table_im = tables(W)
    peak_power = jnp.max(jnp.sum(probe_modes * probe_modes, axis=(0, 1))) + EPSILON
    offsets = positions.reshape(-1, 2)
    measured = amplitudes.reshape(-1, W, W)
    tile_size = object_planes.shape[1]
    extent = tile_size + 2 * M
    place = extent - W
    zero = jnp.zeros((), jnp.int32)
    corner = (zero, offsets[0, 0] + M, offsets[0, 1] + M)
    spread = (zero, place - M - offsets[0, 0], place - M - offsets[0, 1])
    extended = neighbor_sum(object_planes, "row", 1, tile_size, M, 0, extent)
    extended = neighbor_sum(extended, "col", 2, tile_size, M, 0, extent)
    for update in range(ITERS):
        window = lax.dynamic_slice(extended, corner, (2, W, W))
        change = pattern_gradient(window, measured[0], probe_modes, table_re, table_im)
        padded = jnp.pad(change, ((0, 0), (place, place), (place, place)))
        gathered = lax.dynamic_slice(padded, spread, (2, extent, extent))
        if update + 1 < ITERS:
            total = gathered + rows_from_neighbors(change, offsets[0], tile_size, extent)
            total = neighbor_sum(total, "col", 2, tile_size, 0, 0, extent)
            mask = inside_mask(extent, tile_size)
            extended = jnp.where(mask[None], extended + total / peak_power, 0.0)
        else:
            total = neighbor_sum(gathered, "col", 2, tile_size, 0, M, tile_size)
            total = neighbor_sum(total, "row", 1, tile_size, 0, M, tile_size)
            current = extended[:, M : M + tile_size, M : M + tile_size] + total / peak_power
    return current


def solution(mesh):
    in_specs = (
        P(None, "row", "col"),
        P(),
        P("row", "col", None, None),
        P("row", "col", None, None, None),
    )
    out_specs = P(None, "row", "col")
    return jax.shard_map(
        on_device, mesh=mesh, in_specs=in_specs, out_specs=out_specs, check_vma=False
    )
```

```python
import math

import jax
import jax.numpy as jnp
from jax import lax
from jax.experimental import pallas as pl
from jax.experimental.pallas import tpu as pltpu
from jax.sharding import PartitionSpec as P

W = 256
M = 64
ITERS = 2


AMPLITUDE_FLOOR = 0.5
EPSILON = 1e-06


def tables(length):
    counter = jnp.arange(length, dtype=jnp.int32)
    product = counter[:, None] * counter[None, :] % length
    phases = product.astype(jnp.float32) * (2.0 * math.pi / length)
    factor = 1.0 / math.sqrt(length)
    return (
        (jnp.cos(phases) * factor).astype(jnp.bfloat16),
        (-jnp.sin(phases) * factor).astype(jnp.bfloat16),
    )


INTERPRET = False


def gradient_kernel(window_ref, probe_ref, measured_ref, table_re_ref, table_im_ref, out_ref, spectrum_ref):
    modes = probe_ref.shape[1]
    table_re = table_re_ref[...]
    table_im = table_im_ref[...]

    def product(left, right):
        return jnp.dot(left, right, preferred_element_type=jnp.float32)

    def exit_wave(k):
        obj_re = window_ref[0]
        obj_im = window_ref[1]
        probe_re = probe_ref[0, k]
        probe_im = probe_ref[1, k]
        return obj_re * probe_re - obj_im * probe_im, obj_re * probe_im + obj_im * probe_re

    power = None
    for k in range(modes):
        exit_re, exit_im = exit_wave(k)
        exit_re = exit_re.astype(jnp.bfloat16)
        exit_im = exit_im.astype(jnp.bfloat16)
        half_re = (product(table_re, exit_re) - product(table_im, exit_im)).astype(jnp.bfloat16)
        half_im = (product(table_im, exit_re) + product(table_re, exit_im)).astype(jnp.bfloat16)
        spec_re = product(half_re, table_re) - product(half_im, table_im)
        spec_im = product(half_re, table_im) + product(half_im, table_re)
        spectrum_ref[0, k] = spec_re
        spectrum_ref[1, k] = spec_im
        term = spec_re * spec_re + spec_im * spec_im
        power = term if power is None else power + term
    scaling = measured_ref[...] / jnp.maximum(jnp.sqrt(power), AMPLITUDE_FLOOR)
    grad_re = None
    grad_im = None
    for k in range(modes):
        fixed_re = (spectrum_ref[0, k] * scaling).astype(jnp.bfloat16)
        fixed_im = (spectrum_ref[1, k] * scaling).astype(jnp.bfloat16)
        back_re = (product(table_re, fixed_re) + product(table_im, fixed_im)).astype(jnp.bfloat16)
        back_im = (product(table_re, fixed_im) - product(table_im, fixed_re)).astype(jnp.bfloat16)
        revised_re = product(back_re, table_re) + product(back_im, table_im)
        revised_im = product(back_im, table_re) - product(back_re, table_im)
        exit_re, exit_im = exit_wave(k)
        residue_re = revised_re - exit_re
        residue_im = revised_im - exit_im
        probe_re = probe_ref[0, k]
        probe_im = probe_ref[1, k]
        part_re = probe_re * residue_re + probe_im * residue_im
        part_im = probe_re * residue_im - probe_im * residue_re
        grad_re = part_re if grad_re is None else grad_re + part_re
        grad_im = part_im if grad_im is None else grad_im + part_im
    out_ref[0] = grad_re
    out_ref[1] = grad_im


def pattern_gradient(window, measured, probe_modes, table_re, table_im):
    _, modes, rows, cols = probe_modes.shape
    return pl.pallas_call(
        gradient_kernel,
        out_shape=jax.ShapeDtypeStruct((2, rows, cols), jnp.float32),
        scratch_shapes=[pltpu.VMEM((2, modes, rows, cols), jnp.float32)],
        interpret=INTERPRET,
    )(window, probe_modes, measured, table_re, table_im)


def from_neighbor(x, axis, a):
    count = lax.axis_size(axis)
    pairs = [(r, r - a) for r in range(count) if 0 <= r - a < count]
    return lax.ppermute(x, axis, pairs)


def neighbor_sum(frame, axis, dim, step, src_origin, dst_origin, dst_size):
    src_size = frame.shape[dim]
    total = None
    for a in (-1, 0, 1):
        low = max(a * step + src_origin, dst_origin)
        high = min(a * step + src_origin + src_size, dst_origin + dst_size)
        shift = a * step + src_origin
        piece = lax.slice_in_dim(frame, low - shift, high - shift, axis=dim)
        if a != 0:
            piece = from_neighbor(piece, axis, a)
        widths = [(0, 0)] * frame.ndim
        widths[dim] = (low - dst_origin, dst_origin + dst_size - high)
        piece = jnp.pad(piece, widths)
        total = piece if total is None else total + piece
    return total


def rows_from_neighbors(change, offset, tile_size, extent):
    reach = 2 * M
    size = change.shape[1]
    tag_rows = lax.broadcasted_iota(jnp.int32, (2, 8, change.shape[2]), 1)
    tag = jnp.where(tag_rows == 1, offset[1], offset[0]).astype(jnp.float32)
    to_low = jnp.concatenate([change[:, :reach], tag], axis=1)
    to_high = jnp.concatenate([change[:, size - reach :], tag], axis=1)
    from_high = from_neighbor(to_low, "row", 1)
    from_low = from_neighbor(to_high, "row", -1)
    place = extent - W
    total = None
    for got, low_side in ((from_high, False), (from_low, True)):
        strip = got[:, :reach]
        row_at = got[0, reach, 0].astype(jnp.int32)
        col_at = got[0, reach + 1, 0].astype(jnp.int32)
        if low_side:
            top = row_at + M + size - reach - tile_size
            widths = (0, extent)
        else:
            top = row_at + M + tile_size
            widths = (extent, 0)
        padded = jnp.pad(strip, ((0, 0), widths, (place, place)))
        start = widths[0] - top
        piece = lax.dynamic_slice(
            padded, (jnp.zeros((), jnp.int32), start, place - M - col_at), (2, extent, extent)
        )
        total = piece if total is None else total + piece
    return total


def inside_mask(extent, tile_size):
    rows = lax.axis_size("row")
    cols = lax.axis_size("col")
    i = lax.axis_index("row")
    j = lax.axis_index("col")
    pixel = jnp.arange(extent, dtype=jnp.int32)
    row_ok = ((pixel >= M) | (i > 0)) & ((pixel < tile_size + M) | (i < rows - 1))
    col_ok = ((pixel >= M) | (j > 0)) & ((pixel < tile_size + M) | (j < cols - 1))
    return row_ok[:, None] & col_ok[None, :]


def on_device(object_planes, probe_modes, positions, amplitudes):
    table_re, table_im = tables(W)
    peak_power = jnp.max(jnp.sum(probe_modes * probe_modes, axis=(0, 1))) + EPSILON
    offsets = positions.reshape(-1, 2)
    measured = amplitudes.reshape(-1, W, W)
    tile_size = object_planes.shape[1]
    extent = tile_size + 2 * M
    place = extent - W
    zero = jnp.zeros((), jnp.int32)
    corner = (zero, offsets[0, 0] + M, offsets[0, 1] + M)
    spread = (zero, place - M - offsets[0, 0], place - M - offsets[0, 1])
    extended = neighbor_sum(object_planes, "row", 1, tile_size, M, 0, extent)
    extended = neighbor_sum(extended, "col", 2, tile_size, M, 0, extent)
    for update in range(ITERS):
        window = lax.dynamic_slice(extended, corner, (2, W, W))
        change = pattern_gradient(window, measured[0], probe_modes, table_re, table_im)
        padded = jnp.pad(change, ((0, 0), (place, place), (place, place)))
        gathered = lax.dynamic_slice(padded, spread, (2, extent, extent))
        if update + 1 < ITERS:
            total = gathered + rows_from_neighbors(change, offsets[0], tile_size, extent)
            total = neighbor_sum(total, "col", 2, tile_size, 0, 0, extent)
            mask = inside_mask(extent, tile_size)
            extended = jnp.where(mask[None], extended + total / peak_power, 0.0)
        else:
            total = neighbor_sum(gathered, "col", 2, tile_size, 0, M, tile_size)
            total = neighbor_sum(total, "row", 1, tile_size, 0, M, tile_size)
            current = extended[:, M : M + tile_size, M : M + tile_size] + total / peak_power
    return current


def solution(mesh):
    in_specs = (
        P(None, "row", "col"),
        P(),
        P("row", "col", None, None),
        P("row", "col", None, None, None),
    )
    out_specs = P(None, "row", "col")
    return jax.shard_map(
        on_device, mesh=mesh, in_specs=in_specs, out_specs=out_specs, check_vma=False
    )
```

```python
import math

import jax
import jax.numpy as jnp
from jax import lax
from jax.experimental import pallas as pl
from jax.experimental.pallas import tpu as pltpu
from jax.sharding import PartitionSpec as P

W = 256
M = 64
ITERS = 2


AMPLITUDE_FLOOR = 0.5
EPSILON = 1e-06


def tables(length):
    counter = jnp.arange(length, dtype=jnp.int32)
    product = counter[:, None] * counter[None, :] % length
    phases = product.astype(jnp.float32) * (2.0 * math.pi / length)
    factor = 1.0 / math.sqrt(length)
    return (
        (jnp.cos(phases) * factor).astype(jnp.bfloat16),
        (-jnp.sin(phases) * factor).astype(jnp.bfloat16),
    )


INTERPRET = False


def gradient_kernel(window_ref, probe_ref, measured_ref, table_re_ref, table_im_ref, out_ref, spectrum_ref):
    modes = probe_ref.shape[1]
    table_re = table_re_ref[...]
    table_im = table_im_ref[...]

    def product(left, right):
        return jnp.dot(left, right, preferred_element_type=jnp.float32)

    def exit_wave(k):
        obj_re = window_ref[0]
        obj_im = window_ref[1]
        probe_re = probe_ref[0, k]
        probe_im = probe_ref[1, k]
        return obj_re * probe_re - obj_im * probe_im, obj_re * probe_im + obj_im * probe_re

    power = None
    for k in range(modes):
        exit_re, exit_im = exit_wave(k)
        exit_re = exit_re.astype(jnp.bfloat16)
        exit_im = exit_im.astype(jnp.bfloat16)
        half_re = (product(table_re, exit_re) - product(table_im, exit_im)).astype(jnp.bfloat16)
        half_im = (product(table_im, exit_re) + product(table_re, exit_im)).astype(jnp.bfloat16)
        spec_re = product(half_re, table_re) - product(half_im, table_im)
        spec_im = product(half_re, table_im) + product(half_im, table_re)
        spectrum_ref[0, k] = spec_re
        spectrum_ref[1, k] = spec_im
        term = spec_re * spec_re + spec_im * spec_im
        power = term if power is None else power + term
    scaling = measured_ref[...] / jnp.maximum(jnp.sqrt(power), AMPLITUDE_FLOOR)
    grad_re = None
    grad_im = None
    for k in range(modes):
        fixed_re = (spectrum_ref[0, k] * scaling).astype(jnp.bfloat16)
        fixed_im = (spectrum_ref[1, k] * scaling).astype(jnp.bfloat16)
        back_re = (product(table_re, fixed_re) + product(table_im, fixed_im)).astype(jnp.bfloat16)
        back_im = (product(table_re, fixed_im) - product(table_im, fixed_re)).astype(jnp.bfloat16)
        revised_re = product(back_re, table_re) + product(back_im, table_im)
        revised_im = product(back_im, table_re) - product(back_re, table_im)
        exit_re, exit_im = exit_wave(k)
        residue_re = revised_re - exit_re
        residue_im = revised_im - exit_im
        probe_re = probe_ref[0, k]
        probe_im = probe_ref[1, k]
        part_re = probe_re * residue_re + probe_im * residue_im
        part_im = probe_re * residue_im - probe_im * residue_re
        grad_re = part_re if grad_re is None else grad_re + part_re
        grad_im = part_im if grad_im is None else grad_im + part_im
    out_ref[0] = grad_re
    out_ref[1] = grad_im


def pattern_gradient(window, measured, probe_modes, table_re, table_im):
    _, modes, rows, cols = probe_modes.shape
    return pl.pallas_call(
        gradient_kernel,
        out_shape=jax.ShapeDtypeStruct((2, rows, cols), jnp.float32),
        scratch_shapes=[pltpu.VMEM((2, modes, rows, cols), jnp.float32)],
        interpret=INTERPRET,
    )(window, probe_modes, measured, table_re, table_im)


def from_neighbor(x, axis, a):
    count = lax.axis_size(axis)
    pairs = [(r, r - a) for r in range(count) if 0 <= r - a < count]
    return lax.ppermute(x, axis, pairs)


def neighbor_sum(frame, axis, dim, step, src_origin, dst_origin, dst_size):
    src_size = frame.shape[dim]
    total = None
    for a in (-1, 0, 1):
        low = max(a * step + src_origin, dst_origin)
        high = min(a * step + src_origin + src_size, dst_origin + dst_size)
        shift = a * step + src_origin
        piece = lax.slice_in_dim(frame, low - shift, high - shift, axis=dim)
        if a != 0:
            piece = from_neighbor(piece, axis, a)
        widths = [(0, 0)] * frame.ndim
        widths[dim] = (low - dst_origin, dst_origin + dst_size - high)
        piece = jnp.pad(piece, widths)
        total = piece if total is None else total + piece
    return total


def rows_from_neighbors(change, offset, tile_size, reach, dst_origin, dst_size, extent):
    size = change.shape[1]
    tag = jnp.broadcast_to(
        jnp.stack([offset[0], offset[1]] + [offset[0]] * 6).astype(jnp.float32)[None, :, None],
        (2, 8, change.shape[2]),
    )
    to_low = jnp.concatenate([change[:, :reach], tag], axis=1)
    to_high = jnp.concatenate([change[:, size - reach :], tag], axis=1)
    from_high = from_neighbor(to_low, "row", 1)
    from_low = from_neighbor(to_high, "row", -1)
    place = extent - W
    least = -M
    most = tile_size - W + M
    total = None
    for got, base in (
        (from_high, M + tile_size - dst_origin),
        (from_low, M + size - reach - tile_size - dst_origin),
    ):
        strip = got[:, :reach]
        row_at = got[0, reach, 0].astype(jnp.int32)
        col_at = got[0, reach + 1, 0].astype(jnp.int32)
        above = max(0, base + most)
        below = max(0, dst_size - reach - (base + least))
        padded = jnp.pad(strip, ((0, 0), (above, below), (place, place)))
        start = above - (row_at + base)
        piece = lax.dynamic_slice(
            padded, (jnp.zeros((), jnp.int32), start, place - M - col_at), (2, dst_size, extent)
        )
        total = piece if total is None else total + piece
    return total


def inside_mask(extent, tile_size):
    rows = lax.axis_size("row")
    cols = lax.axis_size("col")
    i = lax.axis_index("row")
    j = lax.axis_index("col")
    pixel = jnp.arange(extent, dtype=jnp.int32)
    row_ok = ((pixel >= M) | (i > 0)) & ((pixel < tile_size + M) | (i < rows - 1))
    col_ok = ((pixel >= M) | (j > 0)) & ((pixel < tile_size + M) | (j < cols - 1))
    return row_ok[:, None] & col_ok[None, :]


def on_device(object_planes, probe_modes, positions, amplitudes):
    table_re, table_im = tables(W)
    peak_power = jnp.max(jnp.sum(probe_modes * probe_modes, axis=(0, 1))) + EPSILON
    offsets = positions.reshape(-1, 2)
    measured = amplitudes.reshape(-1, W, W)
    tile_size = object_planes.shape[1]
    extent = tile_size + 2 * M
    place = extent - W
    zero = jnp.zeros((), jnp.int32)
    corner = (zero, offsets[0, 0] + M, offsets[0, 1] + M)
    spread = (zero, place - M - offsets[0, 0], place - M - offsets[0, 1])
    extended = neighbor_sum(object_planes, "row", 1, tile_size, M, 0, extent)
    extended = neighbor_sum(extended, "col", 2, tile_size, M, 0, extent)
    for update in range(ITERS):
        window = lax.dynamic_slice(extended, corner, (2, W, W))
        change = pattern_gradient(window, measured[0], probe_modes, table_re, table_im)
        padded = jnp.pad(change, ((0, 0), (place, place), (place, place)))
        gathered = lax.dynamic_slice(padded, spread, (2, extent, extent))
        if update + 1 < ITERS:
            total = gathered + rows_from_neighbors(change, offsets[0], tile_size, 2 * M, 0, extent, extent)
            total = neighbor_sum(total, "col", 2, tile_size, 0, 0, extent)
            mask = inside_mask(extent, tile_size)
            extended = jnp.where(mask[None], extended + total / peak_power, 0.0)
        else:
            total = gathered[:, M : M + tile_size] + rows_from_neighbors(
                change, offsets[0], tile_size, M, M, tile_size, extent
            )
            total = neighbor_sum(total, "col", 2, tile_size, 0, M, tile_size)
            current = extended[:, M : M + tile_size, M : M + tile_size] + total / peak_power
    return current


def solution(mesh):
    in_specs = (
        P(None, "row", "col"),
        P(),
        P("row", "col", None, None),
        P("row", "col", None, None, None),
    )
    out_specs = P(None, "row", "col")
    return jax.shard_map(
        on_device, mesh=mesh, in_specs=in_specs, out_specs=out_specs, check_vma=False
    )
```

```python
import math

import jax
import jax.numpy as jnp
from jax import lax
from jax.experimental import pallas as pl
from jax.experimental.pallas import tpu as pltpu
from jax.sharding import PartitionSpec as P

W = 256
M = 64
ITERS = 2


AMPLITUDE_FLOOR = 0.5
EPSILON = 1e-06


def tables(length):
    counter = jnp.arange(length, dtype=jnp.int32)
    product = counter[:, None] * counter[None, :] % length
    phases = product.astype(jnp.float32) * (2.0 * math.pi / length)
    factor = 1.0 / math.sqrt(length)
    return (
        (jnp.cos(phases) * factor).astype(jnp.bfloat16),
        (-jnp.sin(phases) * factor).astype(jnp.bfloat16),
    )


INTERPRET = False


def gradient_kernel(window_ref, probe_ref, measured_ref, table_re_ref, table_im_ref, out_ref, spectrum_ref):
    modes = probe_ref.shape[1]
    table_re = table_re_ref[...]
    table_im = table_im_ref[...]

    def product(left, right):
        return jnp.dot(left, right, preferred_element_type=jnp.float32)

    def exit_wave(k):
        obj_re = window_ref[0]
        obj_im = window_ref[1]
        probe_re = probe_ref[0, k]
        probe_im = probe_ref[1, k]
        return obj_re * probe_re - obj_im * probe_im, obj_re * probe_im + obj_im * probe_re

    power = None
    for k in range(modes):
        exit_re, exit_im = exit_wave(k)
        exit_re = exit_re.astype(jnp.bfloat16)
        exit_im = exit_im.astype(jnp.bfloat16)
        half_re = (product(table_re, exit_re) - product(table_im, exit_im)).astype(jnp.bfloat16)
        half_im = (product(table_im, exit_re) + product(table_re, exit_im)).astype(jnp.bfloat16)
        spec_re = product(half_re, table_re) - product(half_im, table_im)
        spec_im = product(half_re, table_im) + product(half_im, table_re)
        spectrum_ref[0, k] = spec_re
        spectrum_ref[1, k] = spec_im
        term = spec_re * spec_re + spec_im * spec_im
        power = term if power is None else power + term
    scaling = measured_ref[...] / jnp.maximum(jnp.sqrt(power), AMPLITUDE_FLOOR)
    grad_re = None
    grad_im = None
    for k in range(modes):
        fixed_re = (spectrum_ref[0, k] * scaling).astype(jnp.bfloat16)
        fixed_im = (spectrum_ref[1, k] * scaling).astype(jnp.bfloat16)
        back_re = (product(table_re, fixed_re) + product(table_im, fixed_im)).astype(jnp.bfloat16)
        back_im = (product(table_re, fixed_im) - product(table_im, fixed_re)).astype(jnp.bfloat16)
        revised_re = product(back_re, table_re) + product(back_im, table_im)
        revised_im = product(back_im, table_re) - product(back_re, table_im)
        exit_re, exit_im = exit_wave(k)
        residue_re = revised_re - exit_re
        residue_im = revised_im - exit_im
        probe_re = probe_ref[0, k]
        probe_im = probe_ref[1, k]
        part_re = probe_re * residue_re + probe_im * residue_im
        part_im = probe_re * residue_im - probe_im * residue_re
        grad_re = part_re if grad_re is None else grad_re + part_re
        grad_im = part_im if grad_im is None else grad_im + part_im
    out_ref[0] = grad_re
    out_ref[1] = grad_im


def pattern_gradient(window, measured, probe_modes, table_re, table_im):
    _, modes, rows, cols = probe_modes.shape
    return pl.pallas_call(
        gradient_kernel,
        out_shape=jax.ShapeDtypeStruct((2, rows, cols), jnp.float32),
        scratch_shapes=[pltpu.VMEM((2, modes, rows, cols), jnp.float32)],
        interpret=INTERPRET,
    )(window, probe_modes, measured, table_re, table_im)


def from_neighbor(x, axis, a):
    count = lax.axis_size(axis)
    pairs = [(r, r - a) for r in range(count) if 0 <= r - a < count]
    return lax.ppermute(x, axis, pairs)


def neighbor_sum(frame, axis, dim, step, src_origin, dst_origin, dst_size):
    src_size = frame.shape[dim]
    total = None
    for a in (-1, 0, 1):
        low = max(a * step + src_origin, dst_origin)
        high = min(a * step + src_origin + src_size, dst_origin + dst_size)
        shift = a * step + src_origin
        piece = lax.slice_in_dim(frame, low - shift, high - shift, axis=dim)
        if a != 0:
            piece = from_neighbor(piece, axis, a)
        widths = [(0, 0)] * frame.ndim
        widths[dim] = (low - dst_origin, dst_origin + dst_size - high)
        piece = jnp.pad(piece, widths)
        total = piece if total is None else total + piece
    return total


def rows_from_neighbors(change, offset, tile_size, extent):
    reach = 2 * M
    size = change.shape[1]
    tag = jnp.broadcast_to(
        jnp.stack([offset[0], offset[1]] + [offset[0]] * 6).astype(jnp.float32)[None, :, None],
        (2, 8, change.shape[2]),
    )
    to_low = jnp.concatenate([change[:, :reach], tag], axis=1)
    to_high = jnp.concatenate([change[:, size - reach :], tag], axis=1)
    from_high = from_neighbor(to_low, "row", 1)
    from_low = from_neighbor(to_high, "row", -1)
    place = extent - W
    total = None
    for got, low_side in ((from_high, False), (from_low, True)):
        strip = got[:, :reach]
        row_at = got[0, reach, 0].astype(jnp.int32)
        col_at = got[0, reach + 1, 0].astype(jnp.int32)
        if low_side:
            top = row_at + M + size - reach - tile_size
            widths = (0, extent)
        else:
            top = row_at + M + tile_size
            widths = (extent, 0)
        padded = jnp.pad(strip, ((0, 0), widths, (place, place)))
        start = widths[0] - top
        piece = lax.dynamic_slice(
            padded, (jnp.zeros((), jnp.int32), start, place - M - col_at), (2, extent, extent)
        )
        total = piece if total is None else total + piece
    return total


def inside_mask(extent, tile_size):
    rows = lax.axis_size("row")
    cols = lax.axis_size("col")
    i = lax.axis_index("row")
    j = lax.axis_index("col")
    pixel = jnp.arange(extent, dtype=jnp.int32)
    row_ok = ((pixel >= M) | (i > 0)) & ((pixel < tile_size + M) | (i < rows - 1))
    col_ok = ((pixel >= M) | (j > 0)) & ((pixel < tile_size + M) | (j < cols - 1))
    return row_ok[:, None] & col_ok[None, :]


def on_device(object_planes, probe_modes, positions, amplitudes):
    table_re, table_im = tables(W)
    peak_power = jnp.max(jnp.sum(probe_modes * probe_modes, axis=(0, 1))) + EPSILON
    offsets = positions.reshape(-1, 2)
    measured = amplitudes.reshape(-1, W, W)
    tile_size = object_planes.shape[1]
    extent = tile_size + 2 * M
    place = extent - W
    zero = jnp.zeros((), jnp.int32)
    corner = (zero, offsets[0, 0] + M, offsets[0, 1] + M)
    spread = (zero, place - M - offsets[0, 0], place - M - offsets[0, 1])
    extended = neighbor_sum(object_planes, "row", 1, tile_size, M, 0, extent)
    extended = neighbor_sum(extended, "col", 2, tile_size, M, 0, extent)
    mask = inside_mask(extent, tile_size)
    grown = None
    for update in range(ITERS):
        window = lax.dynamic_slice(extended, corner, (2, W, W))
        if grown is not None:
            inside = lax.dynamic_slice(mask, corner[1:], (W, W))
            step = lax.dynamic_slice(grown, corner, (2, W, W))
            window = jnp.where(inside[None], window + step, 0.0)
        change = pattern_gradient(window, measured[0], probe_modes, table_re, table_im)
        padded = jnp.pad(change, ((0, 0), (place, place), (place, place)))
        gathered = lax.dynamic_slice(padded, spread, (2, extent, extent))
        if update + 1 < ITERS:
            if grown is not None:
                extended = jnp.where(mask[None], extended + grown, 0.0)
            total = gathered + rows_from_neighbors(change, offsets[0], tile_size, extent)
            total = neighbor_sum(total, "col", 2, tile_size, 0, 0, extent)
            grown = total / peak_power
        else:
            total = neighbor_sum(gathered, "col", 2, tile_size, 0, M, tile_size)
            total = neighbor_sum(total, "row", 1, tile_size, 0, M, tile_size)
            current = extended[:, M : M + tile_size, M : M + tile_size]
            if grown is not None:
                current = current + grown[:, M : M + tile_size, M : M + tile_size]
            current = current + total / peak_power
    return current


def solution(mesh):
    in_specs = (
        P(None, "row", "col"),
        P(),
        P("row", "col", None, None),
        P("row", "col", None, None, None),
    )
    out_specs = P(None, "row", "col")
    return jax.shard_map(
        on_device, mesh=mesh, in_specs=in_specs, out_specs=out_specs, check_vma=False
    )
```

```python
import math

import jax
import jax.numpy as jnp
from jax import lax
from jax.experimental import pallas as pl
from jax.experimental.pallas import tpu as pltpu
from jax.sharding import PartitionSpec as P

W = 256
M = 64
ITERS = 2


AMPLITUDE_FLOOR = 0.5
EPSILON = 1e-06


def tables(length):
    counter = jnp.arange(length, dtype=jnp.int32)
    product = counter[:, None] * counter[None, :] % length
    phases = product.astype(jnp.float32) * (2.0 * math.pi / length)
    factor = 1.0 / math.sqrt(length)
    return (
        (jnp.cos(phases) * factor).astype(jnp.bfloat16),
        (-jnp.sin(phases) * factor).astype(jnp.bfloat16),
    )


INTERPRET = False


def gradient_kernel(window_ref, probe_ref, measured_ref, table_re_ref, table_im_ref, out_ref, spectrum_ref):
    modes = probe_ref.shape[1]
    table_re = table_re_ref[...]
    table_im = table_im_ref[...]

    def product(left, right):
        return jnp.dot(left, right, preferred_element_type=jnp.float32)

    def exit_wave(k):
        obj_re = window_ref[0]
        obj_im = window_ref[1]
        probe_re = probe_ref[0, k]
        probe_im = probe_ref[1, k]
        return obj_re * probe_re - obj_im * probe_im, obj_re * probe_im + obj_im * probe_re

    power = None
    for k in range(modes):
        exit_re, exit_im = exit_wave(k)
        exit_re = exit_re.astype(jnp.bfloat16)
        exit_im = exit_im.astype(jnp.bfloat16)
        half_re = (product(table_re, exit_re) - product(table_im, exit_im)).astype(jnp.bfloat16)
        half_im = (product(table_im, exit_re) + product(table_re, exit_im)).astype(jnp.bfloat16)
        spec_re = product(half_re, table_re) - product(half_im, table_im)
        spec_im = product(half_re, table_im) + product(half_im, table_re)
        spectrum_ref[0, k] = spec_re
        spectrum_ref[1, k] = spec_im
        term = spec_re * spec_re + spec_im * spec_im
        power = term if power is None else power + term
    scaling = measured_ref[...] / jnp.maximum(jnp.sqrt(power), AMPLITUDE_FLOOR)
    grad_re = None
    grad_im = None
    for k in range(modes):
        fixed_re = (spectrum_ref[0, k] * scaling).astype(jnp.bfloat16)
        fixed_im = (spectrum_ref[1, k] * scaling).astype(jnp.bfloat16)
        back_re = (product(table_re, fixed_re) + product(table_im, fixed_im)).astype(jnp.bfloat16)
        back_im = (product(table_re, fixed_im) - product(table_im, fixed_re)).astype(jnp.bfloat16)
        revised_re = product(back_re, table_re) + product(back_im, table_im)
        revised_im = product(back_im, table_re) - product(back_re, table_im)
        exit_re, exit_im = exit_wave(k)
        residue_re = revised_re - exit_re
        residue_im = revised_im - exit_im
        probe_re = probe_ref[0, k]
        probe_im = probe_ref[1, k]
        part_re = probe_re * residue_re + probe_im * residue_im
        part_im = probe_re * residue_im - probe_im * residue_re
        grad_re = part_re if grad_re is None else grad_re + part_re
        grad_im = part_im if grad_im is None else grad_im + part_im
    out_ref[0] = grad_re
    out_ref[1] = grad_im


def pattern_gradient(window, measured, probe_modes, table_re, table_im):
    _, modes, rows, cols = probe_modes.shape
    return pl.pallas_call(
        gradient_kernel,
        out_shape=jax.ShapeDtypeStruct((2, rows, cols), jnp.float32),
        scratch_shapes=[pltpu.VMEM((2, modes, rows, cols), jnp.float32)],
        interpret=INTERPRET,
    )(window, probe_modes, measured, table_re, table_im)


def from_neighbor(x, axis, a):
    count = lax.axis_size(axis)
    pairs = [(r, r - a) for r in range(count) if 0 <= r - a < count]
    return lax.ppermute(x, axis, pairs)


def neighbor_sum(frame, axis, dim, step, src_origin, dst_origin, dst_size):
    src_size = frame.shape[dim]
    total = None
    for a in (-1, 0, 1):
        low = max(a * step + src_origin, dst_origin)
        high = min(a * step + src_origin + src_size, dst_origin + dst_size)
        shift = a * step + src_origin
        piece = lax.slice_in_dim(frame, low - shift, high - shift, axis=dim)
        if a != 0:
            piece = from_neighbor(piece, axis, a)
        widths = [(0, 0)] * frame.ndim
        widths[dim] = (low - dst_origin, dst_origin + dst_size - high)
        piece = jnp.pad(piece, widths)
        total = piece if total is None else total + piece
    return total


def first_rows(object_planes, tag):
    size = object_planes.shape[1]
    to_low = jnp.concatenate([object_planes[:, :M], tag], axis=1)
    to_high = jnp.concatenate([object_planes[:, size - M :], tag], axis=1)
    from_high = from_neighbor(to_low, "row", 1)
    from_low = from_neighbor(to_high, "row", -1)
    rows = jnp.concatenate([from_low[:, :M], object_planes, from_high[:, :M]], axis=1)
    return rows, from_high[:, M:], from_low[:, M:]


def rows_from_neighbors(change, tags, tile_size, extent):
    reach = 2 * M
    size = change.shape[1]
    high_tag, low_tag = tags
    from_high = from_neighbor(change[:, :reach], "row", 1)
    from_low = from_neighbor(change[:, size - reach :], "row", -1)
    place = extent - W
    total = None
    for strip, tag, low_side in ((from_high, high_tag, False), (from_low, low_tag, True)):
        row_at = tag[0, 0, 0].astype(jnp.int32)
        col_at = tag[0, 1, 0].astype(jnp.int32)
        if low_side:
            top = row_at + M + size - reach - tile_size
            widths = (0, extent)
        else:
            top = row_at + M + tile_size
            widths = (extent, 0)
        padded = jnp.pad(strip, ((0, 0), widths, (place, place)))
        start = widths[0] - top
        piece = lax.dynamic_slice(
            padded, (jnp.zeros((), jnp.int32), start, place - M - col_at), (2, extent, extent)
        )
        total = piece if total is None else total + piece
    return total


def inside_mask(extent, tile_size):
    rows = lax.axis_size("row")
    cols = lax.axis_size("col")
    i = lax.axis_index("row")
    j = lax.axis_index("col")
    pixel = jnp.arange(extent, dtype=jnp.int32)
    row_ok = ((pixel >= M) | (i > 0)) & ((pixel < tile_size + M) | (i < rows - 1))
    col_ok = ((pixel >= M) | (j > 0)) & ((pixel < tile_size + M) | (j < cols - 1))
    return row_ok[:, None] & col_ok[None, :]


def on_device(object_planes, probe_modes, positions, amplitudes):
    table_re, table_im = tables(W)
    peak_power = jnp.max(jnp.sum(probe_modes * probe_modes, axis=(0, 1))) + EPSILON
    offsets = positions.reshape(-1, 2)
    measured = amplitudes.reshape(-1, W, W)
    tile_size = object_planes.shape[1]
    extent = tile_size + 2 * M
    place = extent - W
    zero = jnp.zeros((), jnp.int32)
    corner = (zero, offsets[0, 0] + M, offsets[0, 1] + M)
    spread = (zero, place - M - offsets[0, 0], place - M - offsets[0, 1])
    tag = offsets[:1].astype(jnp.float32).reshape(1, 2, 1)
    tag = jnp.pad(jnp.broadcast_to(tag, (2, 2, object_planes.shape[2])), ((0, 0), (0, 6), (0, 0)))
    extended, high_tag, low_tag = first_rows(object_planes, tag)
    extended = neighbor_sum(extended, "col", 2, tile_size, M, 0, extent)
    for update in range(ITERS):
        window = lax.dynamic_slice(extended, corner, (2, W, W))
        change = pattern_gradient(window, measured[0], probe_modes, table_re, table_im)
        padded = jnp.pad(change, ((0, 0), (place, place), (place, place)))
        gathered = lax.dynamic_slice(padded, spread, (2, extent, extent))
        if update + 1 < ITERS:
            total = gathered + rows_from_neighbors(change, (high_tag, low_tag), tile_size, extent)
            total = neighbor_sum(total, "col", 2, tile_size, 0, 0, extent)
            mask = inside_mask(extent, tile_size)
            extended = jnp.where(mask[None], extended + total / peak_power, 0.0)
        else:
            total = neighbor_sum(gathered, "col", 2, tile_size, 0, M, tile_size)
            total = neighbor_sum(total, "row", 1, tile_size, 0, M, tile_size)
            current = extended[:, M : M + tile_size, M : M + tile_size] + total / peak_power
    return current


def solution(mesh):
    in_specs = (
        P(None, "row", "col"),
        P(),
        P("row", "col", None, None),
        P("row", "col", None, None, None),
    )
    out_specs = P(None, "row", "col")
    return jax.shard_map(
        on_device, mesh=mesh, in_specs=in_specs, out_specs=out_specs, check_vma=False
    )
```

```python
import math

import jax
import jax.numpy as jnp
from jax import lax
from jax.experimental import pallas as pl
from jax.experimental.pallas import tpu as pltpu
from jax.sharding import PartitionSpec as P

W = 256
M = 64
ITERS = 2


AMPLITUDE_FLOOR = 0.5
EPSILON = 1e-06


def tables(length):
    counter = jnp.arange(length, dtype=jnp.int32)
    product = counter[:, None] * counter[None, :] % length
    phases = product.astype(jnp.float32) * (2.0 * math.pi / length)
    factor = 1.0 / math.sqrt(length)
    return (
        (jnp.cos(phases) * factor).astype(jnp.bfloat16),
        (-jnp.sin(phases) * factor).astype(jnp.bfloat16),
    )


INTERPRET = False


def gradient_kernel(window_ref, probe_ref, measured_ref, table_re_ref, table_im_ref, out_ref, spectrum_ref):
    modes = probe_ref.shape[1]
    table_re = table_re_ref[...]
    table_im = table_im_ref[...]

    def product(left, right):
        return jnp.dot(left, right, preferred_element_type=jnp.float32)

    def exit_wave(k):
        obj_re = window_ref[0]
        obj_im = window_ref[1]
        probe_re = probe_ref[0, k]
        probe_im = probe_ref[1, k]
        return obj_re * probe_re - obj_im * probe_im, obj_re * probe_im + obj_im * probe_re

    power = None
    for k in range(modes):
        exit_re, exit_im = exit_wave(k)
        exit_re = exit_re.astype(jnp.bfloat16)
        exit_im = exit_im.astype(jnp.bfloat16)
        half_re = (product(table_re, exit_re) - product(table_im, exit_im)).astype(jnp.bfloat16)
        half_im = (product(table_im, exit_re) + product(table_re, exit_im)).astype(jnp.bfloat16)
        spec_re = product(half_re, table_re) - product(half_im, table_im)
        spec_im = product(half_re, table_im) + product(half_im, table_re)
        spectrum_ref[0, k] = spec_re
        spectrum_ref[1, k] = spec_im
        term = spec_re * spec_re + spec_im * spec_im
        power = term if power is None else power + term
    scaling = measured_ref[...] / jnp.maximum(jnp.sqrt(power), AMPLITUDE_FLOOR)
    grad_re = None
    grad_im = None
    for k in range(modes):
        fixed_re = (spectrum_ref[0, k] * scaling).astype(jnp.bfloat16)
        fixed_im = (spectrum_ref[1, k] * scaling).astype(jnp.bfloat16)
        back_re = (product(table_re, fixed_re) + product(table_im, fixed_im)).astype(jnp.bfloat16)
        back_im = (product(table_re, fixed_im) - product(table_im, fixed_re)).astype(jnp.bfloat16)
        revised_re = product(back_re, table_re) + product(back_im, table_im)
        revised_im = product(back_im, table_re) - product(back_re, table_im)
        exit_re, exit_im = exit_wave(k)
        residue_re = revised_re - exit_re
        residue_im = revised_im - exit_im
        probe_re = probe_ref[0, k]
        probe_im = probe_ref[1, k]
        part_re = probe_re * residue_re + probe_im * residue_im
        part_im = probe_re * residue_im - probe_im * residue_re
        grad_re = part_re if grad_re is None else grad_re + part_re
        grad_im = part_im if grad_im is None else grad_im + part_im
    out_ref[0] = grad_re
    out_ref[1] = grad_im


def pattern_gradient(window, measured, probe_modes, table_re, table_im):
    _, modes, rows, cols = probe_modes.shape
    return pl.pallas_call(
        gradient_kernel,
        out_shape=jax.ShapeDtypeStruct((2, rows, cols), jnp.float32),
        scratch_shapes=[pltpu.VMEM((2, modes, rows, cols), jnp.float32)],
        interpret=INTERPRET,
    )(window, probe_modes, measured, table_re, table_im)


def from_neighbor(x, axis, a):
    count = lax.axis_size(axis)
    pairs = [(r, r - a) for r in range(count) if 0 <= r - a < count]
    return lax.ppermute(x, axis, pairs)


def neighbor_sum(frame, axis, dim, step, src_origin, dst_origin, dst_size):
    src_size = frame.shape[dim]
    total = None
    for a in (-1, 0, 1):
        low = max(a * step + src_origin, dst_origin)
        high = min(a * step + src_origin + src_size, dst_origin + dst_size)
        shift = a * step + src_origin
        piece = lax.slice_in_dim(frame, low - shift, high - shift, axis=dim)
        if a != 0:
            piece = from_neighbor(piece, axis, a)
        widths = [(0, 0)] * frame.ndim
        widths[dim] = (low - dst_origin, dst_origin + dst_size - high)
        piece = jnp.pad(piece, widths)
        total = piece if total is None else total + piece
    return total


def rows_from_neighbors(change, offset, tile_size, extent):
    reach = 2 * M
    size = change.shape[1]
    tag = jnp.broadcast_to(
        jnp.stack([offset[0], offset[1]] + [offset[0]] * 6).astype(jnp.float32)[None, :, None],
        (2, 8, change.shape[2]),
    )
    to_low = jnp.concatenate([change[:, :reach], tag], axis=1)
    to_high = jnp.concatenate([change[:, size - reach :], tag], axis=1)
    from_high = from_neighbor(to_low, "row", 1)
    from_low = from_neighbor(to_high, "row", -1)
    place = extent - W
    total = None
    for got, low_side in ((from_high, False), (from_low, True)):
        strip = got[:, :reach]
        row_at = got[0, reach, 0].astype(jnp.int32)
        col_at = got[0, reach + 1, 0].astype(jnp.int32)
        if low_side:
            top = row_at + M + size - reach - tile_size
            widths = (0, extent)
        else:
            top = row_at + M + tile_size
            widths = (extent, 0)
        padded = jnp.pad(strip, ((0, 0), widths, (place, place)))
        start = widths[0] - top
        piece = lax.dynamic_slice(
            padded, (jnp.zeros((), jnp.int32), start, place - M - col_at), (2, extent, extent)
        )
        total = piece if total is None else total + piece
    return total


def inside_mask(extent, tile_size):
    rows = lax.axis_size("row")
    cols = lax.axis_size("col")
    i = lax.axis_index("row")
    j = lax.axis_index("col")
    pixel = jnp.arange(extent, dtype=jnp.int32)
    row_ok = ((pixel >= M) | (i > 0)) & ((pixel < tile_size + M) | (i < rows - 1))
    col_ok = ((pixel >= M) | (j > 0)) & ((pixel < tile_size + M) | (j < cols - 1))
    return row_ok[:, None] & col_ok[None, :]


def on_device(object_planes, probe_modes, positions, amplitudes):
    table_re, table_im = tables(W)
    peak_power = jnp.max(jnp.sum(probe_modes * probe_modes, axis=(0, 1))) + EPSILON
    offsets = positions.reshape(-1, 2)
    measured = amplitudes.reshape(-1, W, W)
    tile_size = object_planes.shape[1]
    extent = tile_size + 2 * M
    place = extent - W
    zero = jnp.zeros((), jnp.int32)
    corner = (zero, offsets[0, 0] + M, offsets[0, 1] + M)
    spread = (zero, place - M - offsets[0, 0], place - M - offsets[0, 1])
    extended = neighbor_sum(object_planes, "row", 1, tile_size, M, 0, extent)
    extended = neighbor_sum(extended, "col", 2, tile_size, M, 0, extent)
    for update in range(ITERS):
        window = lax.dynamic_slice(extended, corner, (2, W, W))
        change = pattern_gradient(window, measured[0], probe_modes, table_re, table_im)
        padded = jnp.pad(change, ((0, 0), (place, place), (place, place)))
        gathered = lax.dynamic_slice(padded, spread, (2, extent, extent))
        if update + 1 < ITERS:
            total = gathered + rows_from_neighbors(change, offsets[0], tile_size, extent)
            total = neighbor_sum(total, "col", 2, tile_size, 0, 0, extent)
            mask = inside_mask(extent, tile_size)
            extended = jnp.where(mask[None], extended + total / peak_power, 0.0)
        else:
            total = neighbor_sum(gathered, "row", 1, tile_size, 0, M, tile_size)
            total = neighbor_sum(total, "col", 2, tile_size, 0, M, tile_size)
            current = extended[:, M : M + tile_size, M : M + tile_size] + total / peak_power
    return current


def solution(mesh):
    in_specs = (
        P(None, "row", "col"),
        P(),
        P("row", "col", None, None),
        P("row", "col", None, None, None),
    )
    out_specs = P(None, "row", "col")
    return jax.shard_map(
        on_device, mesh=mesh, in_specs=in_specs, out_specs=out_specs, check_vma=False
    )
```

```python
import math

import jax
import jax.numpy as jnp
from jax import lax
from jax.experimental import pallas as pl
from jax.experimental.pallas import tpu as pltpu
from jax.sharding import PartitionSpec as P

W = 256
M = 64
ITERS = 2


AMPLITUDE_FLOOR = 0.5
EPSILON = 1e-06


def tables(length):
    counter = jnp.arange(length, dtype=jnp.int32)
    product = counter[:, None] * counter[None, :] % length
    phases = product.astype(jnp.float32) * (2.0 * math.pi / length)
    factor = 1.0 / math.sqrt(length)
    return (
        (jnp.cos(phases) * factor).astype(jnp.bfloat16),
        (-jnp.sin(phases) * factor).astype(jnp.bfloat16),
    )


INTERPRET = False


def gradient_kernel(window_ref, probe_ref, measured_ref, table_re_ref, table_im_ref, out_ref, spectrum_ref,
                    exit_ref):
    modes = probe_ref.shape[1]
    table_re = table_re_ref[...]
    table_im = table_im_ref[...]

    def product(left, right):
        return jnp.dot(left, right, preferred_element_type=jnp.float32)

    def exit_wave(k):
        obj_re = window_ref[0]
        obj_im = window_ref[1]
        probe_re = probe_ref[0, k]
        probe_im = probe_ref[1, k]
        return obj_re * probe_re - obj_im * probe_im, obj_re * probe_im + obj_im * probe_re

    power = None
    for k in range(modes):
        exit_re, exit_im = exit_wave(k)
        exit_ref[0, k] = exit_re
        exit_ref[1, k] = exit_im
        exit_re = exit_re.astype(jnp.bfloat16)
        exit_im = exit_im.astype(jnp.bfloat16)
        half_re = (product(table_re, exit_re) - product(table_im, exit_im)).astype(jnp.bfloat16)
        half_im = (product(table_im, exit_re) + product(table_re, exit_im)).astype(jnp.bfloat16)
        spec_re = product(half_re, table_re) - product(half_im, table_im)
        spec_im = product(half_re, table_im) + product(half_im, table_re)
        spectrum_ref[0, k] = spec_re
        spectrum_ref[1, k] = spec_im
        term = spec_re * spec_re + spec_im * spec_im
        power = term if power is None else power + term
    scaling = measured_ref[...] / jnp.maximum(jnp.sqrt(power), AMPLITUDE_FLOOR)
    grad_re = None
    grad_im = None
    for k in range(modes):
        fixed_re = (spectrum_ref[0, k] * scaling).astype(jnp.bfloat16)
        fixed_im = (spectrum_ref[1, k] * scaling).astype(jnp.bfloat16)
        back_re = (product(table_re, fixed_re) + product(table_im, fixed_im)).astype(jnp.bfloat16)
        back_im = (product(table_re, fixed_im) - product(table_im, fixed_re)).astype(jnp.bfloat16)
        revised_re = product(back_re, table_re) + product(back_im, table_im)
        revised_im = product(back_im, table_re) - product(back_re, table_im)
        residue_re = revised_re - exit_ref[0, k]
        residue_im = revised_im - exit_ref[1, k]
        probe_re = probe_ref[0, k]
        probe_im = probe_ref[1, k]
        part_re = probe_re * residue_re + probe_im * residue_im
        part_im = probe_re * residue_im - probe_im * residue_re
        grad_re = part_re if grad_re is None else grad_re + part_re
        grad_im = part_im if grad_im is None else grad_im + part_im
    out_ref[0] = grad_re
    out_ref[1] = grad_im


def pattern_gradient(window, measured, probe_modes, table_re, table_im):
    _, modes, rows, cols = probe_modes.shape
    return pl.pallas_call(
        gradient_kernel,
        out_shape=jax.ShapeDtypeStruct((2, rows, cols), jnp.float32),
        scratch_shapes=[pltpu.VMEM((2, modes, rows, cols), jnp.float32)] * 2,
        interpret=INTERPRET,
    )(window, probe_modes, measured, table_re, table_im)


def from_neighbor(x, axis, a):
    count = lax.axis_size(axis)
    pairs = [(r, r - a) for r in range(count) if 0 <= r - a < count]
    return lax.ppermute(x, axis, pairs)


def neighbor_sum(frame, axis, dim, step, src_origin, dst_origin, dst_size):
    src_size = frame.shape[dim]
    total = None
    for a in (-1, 0, 1):
        low = max(a * step + src_origin, dst_origin)
        high = min(a * step + src_origin + src_size, dst_origin + dst_size)
        shift = a * step + src_origin
        piece = lax.slice_in_dim(frame, low - shift, high - shift, axis=dim)
        if a != 0:
            piece = from_neighbor(piece, axis, a)
        widths = [(0, 0)] * frame.ndim
        widths[dim] = (low - dst_origin, dst_origin + dst_size - high)
        piece = jnp.pad(piece, widths)
        total = piece if total is None else total + piece
    return total


def rows_from_neighbors(change, offset, tile_size, extent):
    reach = 2 * M
    size = change.shape[1]
    tag = jnp.broadcast_to(
        jnp.stack([offset[0], offset[1]] + [offset[0]] * 6).astype(jnp.float32)[None, :, None],
        (2, 8, change.shape[2]),
    )
    to_low = jnp.concatenate([change[:, :reach], tag], axis=1)
    to_high = jnp.concatenate([change[:, size - reach :], tag], axis=1)
    from_high = from_neighbor(to_low, "row", 1)
    from_low = from_neighbor(to_high, "row", -1)
    place = extent - W
    total = None
    for got, low_side in ((from_high, False), (from_low, True)):
        strip = got[:, :reach]
        row_at = got[0, reach, 0].astype(jnp.int32)
        col_at = got[0, reach + 1, 0].astype(jnp.int32)
        if low_side:
            top = row_at + M + size - reach - tile_size
            widths = (0, extent)
        else:
            top = row_at + M + tile_size
            widths = (extent, 0)
        padded = jnp.pad(strip, ((0, 0), widths, (place, place)))
        start = widths[0] - top
        piece = lax.dynamic_slice(
            padded, (jnp.zeros((), jnp.int32), start, place - M - col_at), (2, extent, extent)
        )
        total = piece if total is None else total + piece
    return total


def inside_mask(extent, tile_size):
    rows = lax.axis_size("row")
    cols = lax.axis_size("col")
    i = lax.axis_index("row")
    j = lax.axis_index("col")
    pixel = jnp.arange(extent, dtype=jnp.int32)
    row_ok = ((pixel >= M) | (i > 0)) & ((pixel < tile_size + M) | (i < rows - 1))
    col_ok = ((pixel >= M) | (j > 0)) & ((pixel < tile_size + M) | (j < cols - 1))
    return row_ok[:, None] & col_ok[None, :]


def on_device(object_planes, probe_modes, positions, amplitudes):
    table_re, table_im = tables(W)
    peak_power = jnp.max(jnp.sum(probe_modes * probe_modes, axis=(0, 1))) + EPSILON
    offsets = positions.reshape(-1, 2)
    measured = amplitudes.reshape(-1, W, W)
    tile_size = object_planes.shape[1]
    extent = tile_size + 2 * M
    place = extent - W
    zero = jnp.zeros((), jnp.int32)
    corner = (zero, offsets[0, 0] + M, offsets[0, 1] + M)
    spread = (zero, place - M - offsets[0, 0], place - M - offsets[0, 1])
    extended = neighbor_sum(object_planes, "row", 1, tile_size, M, 0, extent)
    extended = neighbor_sum(extended, "col", 2, tile_size, M, 0, extent)
    for update in range(ITERS):
        window = lax.dynamic_slice(extended, corner, (2, W, W))
        change = pattern_gradient(window, measured[0], probe_modes, table_re, table_im)
        padded = jnp.pad(change, ((0, 0), (place, place), (place, place)))
        gathered = lax.dynamic_slice(padded, spread, (2, extent, extent))
        if update + 1 < ITERS:
            total = gathered + rows_from_neighbors(change, offsets[0], tile_size, extent)
            total = neighbor_sum(total, "col", 2, tile_size, 0, 0, extent)
            mask = inside_mask(extent, tile_size)
            extended = jnp.where(mask[None], extended + total / peak_power, 0.0)
        else:
            total = neighbor_sum(gathered, "col", 2, tile_size, 0, M, tile_size)
            total = neighbor_sum(total, "row", 1, tile_size, 0, M, tile_size)
            current = extended[:, M : M + tile_size, M : M + tile_size] + total / peak_power
    return current


def solution(mesh):
    in_specs = (
        P(None, "row", "col"),
        P(),
        P("row", "col", None, None),
        P("row", "col", None, None, None),
    )
    out_specs = P(None, "row", "col")
    return jax.shard_map(
        on_device, mesh=mesh, in_specs=in_specs, out_specs=out_specs, check_vma=False
    )
```

```python
import math

import jax
import jax.numpy as jnp
from jax import lax
from jax.experimental import pallas as pl
from jax.experimental.pallas import tpu as pltpu
from jax.sharding import PartitionSpec as P

W = 256
M = 64
ITERS = 2


AMPLITUDE_FLOOR = 0.5
EPSILON = 1e-06


def tables(length):
    counter = jnp.arange(length, dtype=jnp.int32)
    product = counter[:, None] * counter[None, :] % length
    phases = product.astype(jnp.float32) * (2.0 * math.pi / length)
    factor = 1.0 / math.sqrt(length)
    return (
        (jnp.cos(phases) * factor).astype(jnp.bfloat16),
        (-jnp.sin(phases) * factor).astype(jnp.bfloat16),
    )


INTERPRET = False


def gradient_kernel(window_ref, probe_ref, measured_ref, table_re_ref, table_im_ref, out_ref, spectrum_ref,
                    exit_ref):
    modes = probe_ref.shape[1]
    table_re = table_re_ref[...]
    table_im = table_im_ref[...]

    def product(left, right):
        return jnp.dot(left, right, preferred_element_type=jnp.float32)

    def exit_wave(k):
        obj_re = window_ref[0]
        obj_im = window_ref[1]
        probe_re = probe_ref[0, k]
        probe_im = probe_ref[1, k]
        return obj_re * probe_re - obj_im * probe_im, obj_re * probe_im + obj_im * probe_re

    power = None
    for k in range(modes):
        exit_re, exit_im = exit_wave(k)
        exit_ref[0, k] = exit_re
        exit_ref[1, k] = exit_im
        exit_re = exit_re.astype(jnp.bfloat16)
        exit_im = exit_im.astype(jnp.bfloat16)
        half_re = (product(table_re, exit_re) - product(table_im, exit_im)).astype(jnp.bfloat16)
        half_im = (product(table_im, exit_re) + product(table_re, exit_im)).astype(jnp.bfloat16)
        spec_re = product(half_re, table_re) - product(half_im, table_im)
        spec_im = product(half_re, table_im) + product(half_im, table_re)
        spectrum_ref[0, k] = spec_re
        spectrum_ref[1, k] = spec_im
        term = spec_re * spec_re + spec_im * spec_im
        power = term if power is None else power + term
    scaling = measured_ref[...] / jnp.maximum(jnp.sqrt(power), AMPLITUDE_FLOOR)
    grad_re = None
    grad_im = None
    for k in range(modes):
        fixed_re = (spectrum_ref[0, k] * scaling).astype(jnp.bfloat16)
        fixed_im = (spectrum_ref[1, k] * scaling).astype(jnp.bfloat16)
        back_re = (product(table_re, fixed_re) + product(table_im, fixed_im)).astype(jnp.bfloat16)
        back_im = (product(table_re, fixed_im) - product(table_im, fixed_re)).astype(jnp.bfloat16)
        revised_re = product(back_re, table_re) + product(back_im, table_im)
        revised_im = product(back_im, table_re) - product(back_re, table_im)
        residue_re = revised_re - exit_ref[0, k]
        residue_im = revised_im - exit_ref[1, k]
        probe_re = probe_ref[0, k]
        probe_im = probe_ref[1, k]
        part_re = probe_re * residue_re + probe_im * residue_im
        part_im = probe_re * residue_im - probe_im * residue_re
        grad_re = part_re if grad_re is None else grad_re + part_re
        grad_im = part_im if grad_im is None else grad_im + part_im
    out_ref[0] = grad_re
    out_ref[1] = grad_im


def pattern_gradient(window, measured, probe_modes, table_re, table_im):
    _, modes, rows, cols = probe_modes.shape
    return pl.pallas_call(
        gradient_kernel,
        out_shape=jax.ShapeDtypeStruct((2, rows, cols), jnp.float32),
        scratch_shapes=[pltpu.VMEM((2, modes, rows, cols), jnp.float32)] * 2,
        interpret=INTERPRET,
    )(window, probe_modes, measured, table_re, table_im)


def from_neighbor(x, axis, a):
    count = lax.axis_size(axis)
    pairs = [(r, r - a) for r in range(count) if 0 <= r - a < count]
    return lax.ppermute(x, axis, pairs)


def neighbor_sum(frame, axis, dim, step, src_origin, dst_origin, dst_size):
    src_size = frame.shape[dim]
    total = None
    for a in (-1, 0, 1):
        low = max(a * step + src_origin, dst_origin)
        high = min(a * step + src_origin + src_size, dst_origin + dst_size)
        shift = a * step + src_origin
        piece = lax.slice_in_dim(frame, low - shift, high - shift, axis=dim)
        if a != 0:
            piece = from_neighbor(piece, axis, a)
        widths = [(0, 0)] * frame.ndim
        widths[dim] = (low - dst_origin, dst_origin + dst_size - high)
        piece = jnp.pad(piece, widths)
        total = piece if total is None else total + piece
    return total


def rows_from_neighbors(change, offset, tile_size, extent):
    reach = 2 * M
    size = change.shape[1]
    tag = jnp.broadcast_to(
        jnp.stack([offset[0], offset[1]] + [offset[0]] * 6).astype(jnp.float32)[None, :, None],
        (2, 8, change.shape[2]),
    )
    to_low = jnp.concatenate([change[:, :reach], tag], axis=1)
    to_high = jnp.concatenate([change[:, size - reach :], tag], axis=1)
    from_high = from_neighbor(to_low, "row", 1)
    from_low = from_neighbor(to_high, "row", -1)
    place = extent - W
    total = None
    for got, low_side in ((from_high, False), (from_low, True)):
        strip = got[:, :reach]
        row_at = got[0, reach, 0].astype(jnp.int32)
        col_at = got[0, reach + 1, 0].astype(jnp.int32)
        if low_side:
            top = row_at + M + size - reach - tile_size
            widths = (0, extent)
        else:
            top = row_at + M + tile_size
            widths = (extent, 0)
        padded = jnp.pad(strip, ((0, 0), widths, (place, place)))
        start = widths[0] - top
        piece = lax.dynamic_slice(
            padded, (jnp.zeros((), jnp.int32), start, place - M - col_at), (2, extent, extent)
        )
        total = piece if total is None else total + piece
    return total


def first_rows(object_planes):
    size = object_planes.shape[1]
    from_high = from_neighbor(object_planes[:, :M], "row", 1)
    from_low = from_neighbor(object_planes[:, size - M :], "row", -1)
    return jnp.concatenate([from_low, object_planes, from_high], axis=1)


def inside_mask(extent, tile_size):
    rows = lax.axis_size("row")
    cols = lax.axis_size("col")
    i = lax.axis_index("row")
    j = lax.axis_index("col")
    pixel = jnp.arange(extent, dtype=jnp.int32)
    row_ok = ((pixel >= M) | (i > 0)) & ((pixel < tile_size + M) | (i < rows - 1))
    col_ok = ((pixel >= M) | (j > 0)) & ((pixel < tile_size + M) | (j < cols - 1))
    return row_ok[:, None] & col_ok[None, :]


def on_device(object_planes, probe_modes, positions, amplitudes):
    table_re, table_im = tables(W)
    peak_power = jnp.max(jnp.sum(probe_modes * probe_modes, axis=(0, 1))) + EPSILON
    offsets = positions.reshape(-1, 2)
    measured = amplitudes.reshape(-1, W, W)
    tile_size = object_planes.shape[1]
    extent = tile_size + 2 * M
    place = extent - W
    zero = jnp.zeros((), jnp.int32)
    corner = (zero, offsets[0, 0] + M, offsets[0, 1] + M)
    spread = (zero, place - M - offsets[0, 0], place - M - offsets[0, 1])
    extended = first_rows(object_planes)
    extended = neighbor_sum(extended, "col", 2, tile_size, M, 0, extent)
    for update in range(ITERS):
        window = lax.dynamic_slice(extended, corner, (2, W, W))
        change = pattern_gradient(window, measured[0], probe_modes, table_re, table_im)
        padded = jnp.pad(change, ((0, 0), (place, place), (place, place)))
        gathered = lax.dynamic_slice(padded, spread, (2, extent, extent))
        if update + 1 < ITERS:
            total = gathered + rows_from_neighbors(change, offsets[0], tile_size, extent)
            total = neighbor_sum(total, "col", 2, tile_size, 0, 0, extent)
            mask = inside_mask(extent, tile_size)
            extended = jnp.where(mask[None], extended + total / peak_power, 0.0)
        else:
            total = neighbor_sum(gathered, "col", 2, tile_size, 0, M, tile_size)
            total = neighbor_sum(total, "row", 1, tile_size, 0, M, tile_size)
            current = extended[:, M : M + tile_size, M : M + tile_size] + total / peak_power
    return current


def solution(mesh):
    in_specs = (
        P(None, "row", "col"),
        P(),
        P("row", "col", None, None),
        P("row", "col", None, None, None),
    )
    out_specs = P(None, "row", "col")
    return jax.shard_map(
        on_device, mesh=mesh, in_specs=in_specs, out_specs=out_specs, check_vma=False
    )
```

```python
import math

import jax
import jax.numpy as jnp
from jax import lax
from jax.experimental import pallas as pl
from jax.experimental.pallas import tpu as pltpu
from jax.sharding import PartitionSpec as P

W = 256
M = 64
ITERS = 2


AMPLITUDE_FLOOR = 0.5
EPSILON = 1e-06


def tables(length):
    counter = jnp.arange(length, dtype=jnp.int32)
    product = counter[:, None] * counter[None, :] % length
    phases = product.astype(jnp.float32) * (2.0 * math.pi / length)
    factor = 1.0 / math.sqrt(length)
    return (
        (jnp.cos(phases) * factor).astype(jnp.bfloat16),
        (-jnp.sin(phases) * factor).astype(jnp.bfloat16),
    )


INTERPRET = False


def gradient_kernel(window_ref, probe_hbm, measured_ref, table_re_ref, table_im_ref, out_ref, spectrum_ref,
                    exit_ref, probe_ref, arrived):
    modes = probe_ref.shape[1]
    copies = [
        [pltpu.make_async_copy(probe_hbm.at[p, k], probe_ref.at[p, k], arrived.at[p, k]) for p in range(2)]
        for k in range(modes)
    ]
    for pair in copies:
        for copy in pair:
            copy.start()
    table_re = table_re_ref[...]
    table_im = table_im_ref[...]

    def product(left, right):
        return jnp.dot(left, right, preferred_element_type=jnp.float32)

    def exit_wave(k):
        obj_re = window_ref[0]
        obj_im = window_ref[1]
        probe_re = probe_ref[0, k]
        probe_im = probe_ref[1, k]
        return obj_re * probe_re - obj_im * probe_im, obj_re * probe_im + obj_im * probe_re

    power = None
    for k in range(modes):
        for copy in copies[k]:
            copy.wait()
        exit_re, exit_im = exit_wave(k)
        exit_ref[0, k] = exit_re
        exit_ref[1, k] = exit_im
        exit_re = exit_re.astype(jnp.bfloat16)
        exit_im = exit_im.astype(jnp.bfloat16)
        half_re = (product(table_re, exit_re) - product(table_im, exit_im)).astype(jnp.bfloat16)
        half_im = (product(table_im, exit_re) + product(table_re, exit_im)).astype(jnp.bfloat16)
        spec_re = product(half_re, table_re) - product(half_im, table_im)
        spec_im = product(half_re, table_im) + product(half_im, table_re)
        spectrum_ref[0, k] = spec_re
        spectrum_ref[1, k] = spec_im
        term = spec_re * spec_re + spec_im * spec_im
        power = term if power is None else power + term
    scaling = measured_ref[...] / jnp.maximum(jnp.sqrt(power), AMPLITUDE_FLOOR)
    grad_re = None
    grad_im = None
    for k in range(modes):
        fixed_re = (spectrum_ref[0, k] * scaling).astype(jnp.bfloat16)
        fixed_im = (spectrum_ref[1, k] * scaling).astype(jnp.bfloat16)
        back_re = (product(table_re, fixed_re) + product(table_im, fixed_im)).astype(jnp.bfloat16)
        back_im = (product(table_re, fixed_im) - product(table_im, fixed_re)).astype(jnp.bfloat16)
        revised_re = product(back_re, table_re) + product(back_im, table_im)
        revised_im = product(back_im, table_re) - product(back_re, table_im)
        residue_re = revised_re - exit_ref[0, k]
        residue_im = revised_im - exit_ref[1, k]
        probe_re = probe_ref[0, k]
        probe_im = probe_ref[1, k]
        part_re = probe_re * residue_re + probe_im * residue_im
        part_im = probe_re * residue_im - probe_im * residue_re
        grad_re = part_re if grad_re is None else grad_re + part_re
        grad_im = part_im if grad_im is None else grad_im + part_im
    out_ref[0] = grad_re
    out_ref[1] = grad_im


def pattern_gradient(window, measured, probe_modes, table_re, table_im):
    _, modes, rows, cols = probe_modes.shape
    return pl.pallas_call(
        gradient_kernel,
        out_shape=jax.ShapeDtypeStruct((2, rows, cols), jnp.float32),
        in_specs=[
            pl.BlockSpec(memory_space=pltpu.VMEM),
            pl.BlockSpec(memory_space=pl.ANY),
            pl.BlockSpec(memory_space=pltpu.VMEM),
            pl.BlockSpec(memory_space=pltpu.VMEM),
            pl.BlockSpec(memory_space=pltpu.VMEM),
        ],
        scratch_shapes=[pltpu.VMEM((2, modes, rows, cols), jnp.float32)] * 3
        + [pltpu.SemaphoreType.DMA((2, modes))],
        interpret=INTERPRET,
    )(window, probe_modes, measured, table_re, table_im)


def from_neighbor(x, axis, a):
    count = lax.axis_size(axis)
    pairs = [(r, r - a) for r in range(count) if 0 <= r - a < count]
    return lax.ppermute(x, axis, pairs)


def neighbor_sum(frame, axis, dim, step, src_origin, dst_origin, dst_size):
    src_size = frame.shape[dim]
    total = None
    for a in (-1, 0, 1):
        low = max(a * step + src_origin, dst_origin)
        high = min(a * step + src_origin + src_size, dst_origin + dst_size)
        shift = a * step + src_origin
        piece = lax.slice_in_dim(frame, low - shift, high - shift, axis=dim)
        if a != 0:
            piece = from_neighbor(piece, axis, a)
        widths = [(0, 0)] * frame.ndim
        widths[dim] = (low - dst_origin, dst_origin + dst_size - high)
        piece = jnp.pad(piece, widths)
        total = piece if total is None else total + piece
    return total


def rows_from_neighbors(change, offset, tile_size, extent):
    reach = 2 * M
    size = change.shape[1]
    tag = jnp.broadcast_to(
        jnp.stack([offset[0], offset[1]] + [offset[0]] * 6).astype(jnp.float32)[None, :, None],
        (2, 8, change.shape[2]),
    )
    to_low = jnp.concatenate([change[:, :reach], tag], axis=1)
    to_high = jnp.concatenate([change[:, size - reach :], tag], axis=1)
    from_high = from_neighbor(to_low, "row", 1)
    from_low = from_neighbor(to_high, "row", -1)
    place = extent - W
    total = None
    for got, low_side in ((from_high, False), (from_low, True)):
        strip = got[:, :reach]
        row_at = got[0, reach, 0].astype(jnp.int32)
        col_at = got[0, reach + 1, 0].astype(jnp.int32)
        if low_side:
            top = row_at + M + size - reach - tile_size
            widths = (0, extent)
        else:
            top = row_at + M + tile_size
            widths = (extent, 0)
        padded = jnp.pad(strip, ((0, 0), widths, (place, place)))
        start = widths[0] - top
        piece = lax.dynamic_slice(
            padded, (jnp.zeros((), jnp.int32), start, place - M - col_at), (2, extent, extent)
        )
        total = piece if total is None else total + piece
    return total


def inside_mask(extent, tile_size):
    rows = lax.axis_size("row")
    cols = lax.axis_size("col")
    i = lax.axis_index("row")
    j = lax.axis_index("col")
    pixel = jnp.arange(extent, dtype=jnp.int32)
    row_ok = ((pixel >= M) | (i > 0)) & ((pixel < tile_size + M) | (i < rows - 1))
    col_ok = ((pixel >= M) | (j > 0)) & ((pixel < tile_size + M) | (j < cols - 1))
    return row_ok[:, None] & col_ok[None, :]


def on_device(object_planes, probe_modes, positions, amplitudes):
    table_re, table_im = tables(W)
    peak_power = jnp.max(jnp.sum(probe_modes * probe_modes, axis=(0, 1))) + EPSILON
    offsets = positions.reshape(-1, 2)
    measured = amplitudes.reshape(-1, W, W)
    tile_size = object_planes.shape[1]
    extent = tile_size + 2 * M
    place = extent - W
    zero = jnp.zeros((), jnp.int32)
    corner = (zero, offsets[0, 0] + M, offsets[0, 1] + M)
    spread = (zero, place - M - offsets[0, 0], place - M - offsets[0, 1])
    extended = neighbor_sum(object_planes, "row", 1, tile_size, M, 0, extent)
    extended = neighbor_sum(extended, "col", 2, tile_size, M, 0, extent)
    for update in range(ITERS):
        window = lax.dynamic_slice(extended, corner, (2, W, W))
        change = pattern_gradient(window, measured[0], probe_modes, table_re, table_im)
        padded = jnp.pad(change, ((0, 0), (place, place), (place, place)))
        gathered = lax.dynamic_slice(padded, spread, (2, extent, extent))
        if update + 1 < ITERS:
            total = gathered + rows_from_neighbors(change, offsets[0], tile_size, extent)
            total = neighbor_sum(total, "col", 2, tile_size, 0, 0, extent)
            mask = inside_mask(extent, tile_size)
            extended = jnp.where(mask[None], extended + total / peak_power, 0.0)
        else:
            total = neighbor_sum(gathered, "col", 2, tile_size, 0, M, tile_size)
            total = neighbor_sum(total, "row", 1, tile_size, 0, M, tile_size)
            current = extended[:, M : M + tile_size, M : M + tile_size] + total / peak_power
    return current


def solution(mesh):
    in_specs = (
        P(None, "row", "col"),
        P(),
        P("row", "col", None, None),
        P("row", "col", None, None, None),
    )
    out_specs = P(None, "row", "col")
    return jax.shard_map(
        on_device, mesh=mesh, in_specs=in_specs, out_specs=out_specs, check_vma=False
    )
```

```python
import math

import jax
import jax.numpy as jnp
from jax import lax
from jax.experimental import pallas as pl
from jax.experimental.pallas import tpu as pltpu
from jax.sharding import PartitionSpec as P

W = 256
M = 64
ITERS = 2


AMPLITUDE_FLOOR = 0.5
EPSILON = 1e-06


def tables(length):
    counter = jnp.arange(length, dtype=jnp.int32)
    product = counter[:, None] * counter[None, :] % length
    phases = product.astype(jnp.float32) * (2.0 * math.pi / length)
    factor = 1.0 / math.sqrt(length)
    return (
        (jnp.cos(phases) * factor).astype(jnp.bfloat16),
        (-jnp.sin(phases) * factor).astype(jnp.bfloat16),
    )


INTERPRET = False


def gradient_kernel(window_ref, probe_ref, measured_ref, table_re_ref, table_im_ref, out_ref, spectrum_ref,
                    exit_ref):
    modes = probe_ref.shape[1]
    table_re = table_re_ref[...]
    table_im = table_im_ref[...]

    def product(left, right):
        return jnp.dot(left, right, preferred_element_type=jnp.float32)

    def exit_wave(k):
        obj_re = window_ref[0]
        obj_im = window_ref[1]
        probe_re = probe_ref[0, k]
        probe_im = probe_ref[1, k]
        return obj_re * probe_re - obj_im * probe_im, obj_re * probe_im + obj_im * probe_re

    power = None
    for k in range(modes):
        exit_re, exit_im = exit_wave(k)
        exit_ref[0, k] = exit_re
        exit_ref[1, k] = exit_im
        exit_re = exit_re.astype(jnp.bfloat16)
        exit_im = exit_im.astype(jnp.bfloat16)
        half_re = (product(table_re, exit_re) - product(table_im, exit_im)).astype(jnp.bfloat16)
        half_im = (product(table_im, exit_re) + product(table_re, exit_im)).astype(jnp.bfloat16)
        spec_re = product(half_re, table_re) - product(half_im, table_im)
        spec_im = product(half_re, table_im) + product(half_im, table_re)
        spectrum_ref[0, k] = spec_re
        spectrum_ref[1, k] = spec_im
        term = spec_re * spec_re + spec_im * spec_im
        power = term if power is None else power + term
    scaling = measured_ref[...] / jnp.maximum(jnp.sqrt(power), AMPLITUDE_FLOOR)
    grad_re = None
    grad_im = None
    for k in range(modes):
        fixed_re = (spectrum_ref[0, k] * scaling).astype(jnp.bfloat16)
        fixed_im = (spectrum_ref[1, k] * scaling).astype(jnp.bfloat16)
        back_re = (product(table_re, fixed_re) + product(table_im, fixed_im)).astype(jnp.bfloat16)
        back_im = (product(table_re, fixed_im) - product(table_im, fixed_re)).astype(jnp.bfloat16)
        revised_re = product(back_re, table_re) + product(back_im, table_im)
        revised_im = product(back_im, table_re) - product(back_re, table_im)
        residue_re = revised_re - exit_ref[0, k]
        residue_im = revised_im - exit_ref[1, k]
        probe_re = probe_ref[0, k]
        probe_im = probe_ref[1, k]
        part_re = probe_re * residue_re + probe_im * residue_im
        part_im = probe_re * residue_im - probe_im * residue_re
        grad_re = part_re if grad_re is None else grad_re + part_re
        grad_im = part_im if grad_im is None else grad_im + part_im
    out_ref[0] = grad_re
    out_ref[1] = grad_im


def pattern_gradient(window, measured, probe_modes, table_re, table_im):
    _, modes, rows, cols = probe_modes.shape
    return pl.pallas_call(
        gradient_kernel,
        out_shape=jax.ShapeDtypeStruct((2, rows, cols), jnp.float32),
        scratch_shapes=[pltpu.VMEM((2, modes, rows, cols), jnp.float32)] * 2,
        interpret=INTERPRET,
    )(window, probe_modes, measured, table_re, table_im)


def from_neighbor(x, axis, a):
    count = lax.axis_size(axis)
    pairs = [(r, r - a) for r in range(count) if 0 <= r - a < count]
    return lax.ppermute(x, axis, pairs)


def neighbor_sum(frame, axis, dim, step, src_origin, dst_origin, dst_size):
    src_size = frame.shape[dim]
    total = None
    for a in (-1, 0, 1):
        low = max(a * step + src_origin, dst_origin)
        high = min(a * step + src_origin + src_size, dst_origin + dst_size)
        shift = a * step + src_origin
        piece = lax.slice_in_dim(frame, low - shift, high - shift, axis=dim)
        if a != 0:
            piece = from_neighbor(piece, axis, a)
        widths = [(0, 0)] * frame.ndim
        widths[dim] = (low - dst_origin, dst_origin + dst_size - high)
        piece = jnp.pad(piece, widths)
        total = piece if total is None else total + piece
    return total


def first_rows(object_planes, tag):
    size = object_planes.shape[1]
    to_low = jnp.concatenate([object_planes[:, :M], tag], axis=1)
    to_high = jnp.concatenate([object_planes[:, size - M :], tag], axis=1)
    from_high = from_neighbor(to_low, "row", 1)
    from_low = from_neighbor(to_high, "row", -1)
    rows = jnp.concatenate([from_low[:, :M], object_planes, from_high[:, :M]], axis=1)
    return rows, from_high[:, M:], from_low[:, M:]


def rows_from_neighbors(change, tags, tile_size, extent):
    reach = 2 * M
    size = change.shape[1]
    high_tag, low_tag = tags
    from_high = from_neighbor(change[:, :reach], "row", 1)
    from_low = from_neighbor(change[:, size - reach :], "row", -1)
    place = extent - W
    total = None
    for strip, tag, low_side in ((from_high, high_tag, False), (from_low, low_tag, True)):
        row_at = tag[0, 0, 0].astype(jnp.int32)
        col_at = tag[0, 1, 0].astype(jnp.int32)
        if low_side:
            top = row_at + M + size - reach - tile_size
            widths = (0, extent)
        else:
            top = row_at + M + tile_size
            widths = (extent, 0)
        padded = jnp.pad(strip, ((0, 0), widths, (place, place)))
        start = widths[0] - top
        piece = lax.dynamic_slice(
            padded, (jnp.zeros((), jnp.int32), start, place - M - col_at), (2, extent, extent)
        )
        total = piece if total is None else total + piece
    return total


def inside_mask(extent, tile_size):
    rows = lax.axis_size("row")
    cols = lax.axis_size("col")
    i = lax.axis_index("row")
    j = lax.axis_index("col")
    pixel = jnp.arange(extent, dtype=jnp.int32)
    row_ok = ((pixel >= M) | (i > 0)) & ((pixel < tile_size + M) | (i < rows - 1))
    col_ok = ((pixel >= M) | (j > 0)) & ((pixel < tile_size + M) | (j < cols - 1))
    return row_ok[:, None] & col_ok[None, :]


def on_device(object_planes, probe_modes, positions, amplitudes):
    table_re, table_im = tables(W)
    peak_power = jnp.max(jnp.sum(probe_modes * probe_modes, axis=(0, 1))) + EPSILON
    offsets = positions.reshape(-1, 2)
    measured = amplitudes.reshape(-1, W, W)
    tile_size = object_planes.shape[1]
    extent = tile_size + 2 * M
    place = extent - W
    zero = jnp.zeros((), jnp.int32)
    corner = (zero, offsets[0, 0] + M, offsets[0, 1] + M)
    spread = (zero, place - M - offsets[0, 0], place - M - offsets[0, 1])
    tag = offsets[:1].astype(jnp.float32).reshape(1, 2, 1)
    tag = jnp.pad(jnp.broadcast_to(tag, (2, 2, object_planes.shape[2])), ((0, 0), (0, 6), (0, 0)))
    extended, high_tag, low_tag = first_rows(object_planes, tag)
    extended = neighbor_sum(extended, "col", 2, tile_size, M, 0, extent)
    for update in range(ITERS):
        window = lax.dynamic_slice(extended, corner, (2, W, W))
        change = pattern_gradient(window, measured[0], probe_modes, table_re, table_im)
        padded = jnp.pad(change, ((0, 0), (place, place), (place, place)))
        gathered = lax.dynamic_slice(padded, spread, (2, extent, extent))
        if update + 1 < ITERS:
            total = gathered + rows_from_neighbors(change, (high_tag, low_tag), tile_size, extent)
            total = neighbor_sum(total, "col", 2, tile_size, 0, 0, extent)
            mask = inside_mask(extent, tile_size)
            extended = jnp.where(mask[None], extended + total / peak_power, 0.0)
        else:
            total = neighbor_sum(gathered, "col", 2, tile_size, 0, M, tile_size)
            total = neighbor_sum(total, "row", 1, tile_size, 0, M, tile_size)
            current = extended[:, M : M + tile_size, M : M + tile_size] + total / peak_power
    return current


def solution(mesh):
    in_specs = (
        P(None, "row", "col"),
        P(),
        P("row", "col", None, None),
        P("row", "col", None, None, None),
    )
    out_specs = P(None, "row", "col")
    return jax.shard_map(
        on_device, mesh=mesh, in_specs=in_specs, out_specs=out_specs, check_vma=False
    )
```

```python
import math

import jax
import jax.numpy as jnp
from jax import lax
from jax.experimental import pallas as pl
from jax.experimental.pallas import tpu as pltpu
from jax.sharding import PartitionSpec as P

W = 256
M = 64
ITERS = 2


AMPLITUDE_FLOOR = 0.5
EPSILON = 1e-06


def tables(length):
    counter = jnp.arange(length, dtype=jnp.int32)
    product = counter[:, None] * counter[None, :] % length
    phases = product.astype(jnp.float32) * (2.0 * math.pi / length)
    factor = 1.0 / math.sqrt(length)
    return (
        (jnp.cos(phases) * factor).astype(jnp.bfloat16),
        (-jnp.sin(phases) * factor).astype(jnp.bfloat16),
    )


INTERPRET = False


def gradient_kernel(window_ref, probe_ref, measured_ref, table_re_ref, table_im_ref, out_ref, spectrum_ref):
    modes = probe_ref.shape[1]
    table_re = table_re_ref[...]
    table_im = table_im_ref[...]

    def product(left, right):
        return jnp.dot(left, right, preferred_element_type=jnp.float32)

    def exit_wave(k):
        obj_re = window_ref[0]
        obj_im = window_ref[1]
        probe_re = probe_ref[0, k]
        probe_im = probe_ref[1, k]
        return obj_re * probe_re - obj_im * probe_im, obj_re * probe_im + obj_im * probe_re

    power = None
    for k in range(modes):
        exit_re, exit_im = exit_wave(k)
        exit_re = exit_re.astype(jnp.bfloat16)
        exit_im = exit_im.astype(jnp.bfloat16)
        half_re = (product(table_re, exit_re) - product(table_im, exit_im)).astype(jnp.bfloat16)
        half_im = (product(table_im, exit_re) + product(table_re, exit_im)).astype(jnp.bfloat16)
        spec_re = product(half_re, table_re) - product(half_im, table_im)
        spec_im = product(half_re, table_im) + product(half_im, table_re)
        spectrum_ref[0, k] = spec_re
        spectrum_ref[1, k] = spec_im
        term = spec_re * spec_re + spec_im * spec_im
        power = term if power is None else power + term
    scaling = measured_ref[...] / jnp.maximum(jnp.sqrt(power), AMPLITUDE_FLOOR)
    grad_re = None
    grad_im = None
    for k in range(modes):
        fixed_re = (spectrum_ref[0, k] * scaling).astype(jnp.bfloat16)
        fixed_im = (spectrum_ref[1, k] * scaling).astype(jnp.bfloat16)
        back_re = (product(table_re, fixed_re) + product(table_im, fixed_im)).astype(jnp.bfloat16)
        back_im = (product(table_re, fixed_im) - product(table_im, fixed_re)).astype(jnp.bfloat16)
        revised_re = product(back_re, table_re) + product(back_im, table_im)
        revised_im = product(back_im, table_re) - product(back_re, table_im)
        exit_re, exit_im = exit_wave(k)
        residue_re = revised_re - exit_re
        residue_im = revised_im - exit_im
        probe_re = probe_ref[0, k]
        probe_im = probe_ref[1, k]
        part_re = probe_re * residue_re + probe_im * residue_im
        part_im = probe_re * residue_im - probe_im * residue_re
        grad_re = part_re if grad_re is None else grad_re + part_re
        grad_im = part_im if grad_im is None else grad_im + part_im
    out_ref[0] = grad_re
    out_ref[1] = grad_im


def pattern_gradient(window, measured, probe_modes, table_re, table_im):
    _, modes, rows, cols = probe_modes.shape
    return pl.pallas_call(
        gradient_kernel,
        out_shape=jax.ShapeDtypeStruct((2, rows, cols), jnp.float32),
        scratch_shapes=[pltpu.VMEM((2, modes, rows, cols), jnp.float32)],
        interpret=INTERPRET,
    )(window, probe_modes, measured, table_re, table_im)


def from_neighbor(x, axis, a):
    count = lax.axis_size(axis)
    pairs = [(r, r - a) for r in range(count) if 0 <= r - a < count]
    return lax.ppermute(x, axis, pairs)


def neighbor_sum(frame, axis, dim, step, src_origin, dst_origin, dst_size):
    src_size = frame.shape[dim]
    total = None
    for a in (-1, 0, 1):
        low = max(a * step + src_origin, dst_origin)
        high = min(a * step + src_origin + src_size, dst_origin + dst_size)
        shift = a * step + src_origin
        piece = lax.slice_in_dim(frame, low - shift, high - shift, axis=dim)
        if a != 0:
            piece = from_neighbor(piece, axis, a)
        widths = [(0, 0)] * frame.ndim
        widths[dim] = (low - dst_origin, dst_origin + dst_size - high)
        piece = jnp.pad(piece, widths)
        total = piece if total is None else total + piece
    return total


def rows_from_neighbors(change, offset, tile_size, extent):
    reach = 2 * M
    size = change.shape[1]
    tag = jnp.broadcast_to(
        jnp.stack([offset[0], offset[1]] + [offset[0]] * 6).astype(jnp.float32)[None, :, None],
        (2, 8, change.shape[2]),
    )
    to_low = jnp.concatenate([change[:, :reach], tag], axis=1)
    to_high = jnp.concatenate([change[:, size - reach :], tag], axis=1)
    from_high = from_neighbor(to_low, "row", 1)
    from_low = from_neighbor(to_high, "row", -1)
    place = extent - W
    total = None
    for got, low_side in ((from_high, False), (from_low, True)):
        strip = got[:, :reach]
        row_at = got[0, reach, 0].astype(jnp.int32)
        col_at = got[0, reach + 1, 0].astype(jnp.int32)
        if low_side:
            top = row_at + M + size - reach - tile_size
            widths = (0, extent)
        else:
            top = row_at + M + tile_size
            widths = (extent, 0)
        padded = jnp.pad(strip, ((0, 0), widths, (place, place)))
        start = widths[0] - top
        piece = lax.dynamic_slice(
            padded, (jnp.zeros((), jnp.int32), start, place - M - col_at), (2, extent, extent)
        )
        total = piece if total is None else total + piece
    return total


def inside_mask(extent, tile_size):
    rows = lax.axis_size("row")
    cols = lax.axis_size("col")
    i = lax.axis_index("row")
    j = lax.axis_index("col")
    pixel = jnp.arange(extent, dtype=jnp.int32)
    row_ok = ((pixel >= M) | (i > 0)) & ((pixel < tile_size + M) | (i < rows - 1))
    col_ok = ((pixel >= M) | (j > 0)) & ((pixel < tile_size + M) | (j < cols - 1))
    return row_ok[:, None] & col_ok[None, :]


def on_device(object_planes, probe_modes, positions, amplitudes):
    table_re, table_im = tables(W)
    peak_power = jnp.max(jnp.sum(probe_modes * probe_modes, axis=(0, 1))) + EPSILON
    offsets = positions.reshape(-1, 2)
    measured = amplitudes.reshape(-1, W, W)
    tile_size = object_planes.shape[1]
    extent = tile_size + 2 * M
    place = extent - W
    zero = jnp.zeros((), jnp.int32)
    corner = (zero, offsets[0, 0] + M, offsets[0, 1] + M)
    spread = (zero, place - M - offsets[0, 0], place - M - offsets[0, 1])
    extended = neighbor_sum(object_planes, "col", 2, tile_size, M, 0, extent)
    extended = neighbor_sum(extended, "row", 1, tile_size, M, 0, extent)
    for update in range(ITERS):
        window = lax.dynamic_slice(extended, corner, (2, W, W))
        change = pattern_gradient(window, measured[0], probe_modes, table_re, table_im)
        padded = jnp.pad(change, ((0, 0), (place, place), (place, place)))
        gathered = lax.dynamic_slice(padded, spread, (2, extent, extent))
        if update + 1 < ITERS:
            total = gathered + rows_from_neighbors(change, offsets[0], tile_size, extent)
            total = neighbor_sum(total, "col", 2, tile_size, 0, 0, extent)
            mask = inside_mask(extent, tile_size)
            extended = jnp.where(mask[None], extended + total / peak_power, 0.0)
        else:
            total = neighbor_sum(gathered, "col", 2, tile_size, 0, M, tile_size)
            total = neighbor_sum(total, "row", 1, tile_size, 0, M, tile_size)
            current = extended[:, M : M + tile_size, M : M + tile_size] + total / peak_power
    return current


def solution(mesh):
    in_specs = (
        P(None, "row", "col"),
        P(),
        P("row", "col", None, None),
        P("row", "col", None, None, None),
    )
    out_specs = P(None, "row", "col")
    return jax.shard_map(
        on_device, mesh=mesh, in_specs=in_specs, out_specs=out_specs, check_vma=False
    )
```
